128 devices in a mesh: expert: 64 (over x, y, z), replica: 2 (over core).
Axes of the slice: x: 4, y: 4, z: 4, core: 2. Of those that a mesh axis runs over, the one named last changes fastest.
Arguments:
- x_quant: bfloat16 [16384, 2048], P(('expert', 'replica')), may hold values from -6 to 6
- x_scale: float32 [16384, 16], P(('expert', 'replica')), may hold values from 0.3 to 3
- out_grad: bfloat16 [16384, 2048], P(('expert', 'replica')), may hold values from -6 to 6
- expert_ids: int32 [16384, 8], P(('expert', 'replica')), may hold values from 0 to 63, all different within a row; in each aligned block of 128 rows (0 to 127, 128 to 255, ...) at most 20 rows name the same one
- gate_fixed: int32 [16384, 8], P(('expert', 'replica')), may hold values from 1024 to 16383
- w_gate: bfloat16 [64, 2048, 768], P('expert'), may hold values from -0.125 to 0.125
- s_gate: float32 [64, 16, 6], P('expert'), may hold values from 0.3 to 3
- w_up: bfloat16 [64, 2048, 768], P('expert'), may hold values from -0.125 to 0.125
- s_up: float32 [64, 16, 6], P('expert'), may hold values from 0.3 to 3
- w_down: bfloat16 [64, 768, 2048], P('expert'), may hold values from -0.21875 to 0.21875
- s_down: float32 [64, 6, 16], P('expert'), may hold values from 0.3 to 3
Outputs:
- grad_input: bfloat16 [16384, 2048], P(('expert', 'replica'))
- grad_gate: bfloat16 [64, 2048, 768], P('expert', None, 'replica')
- grad_up: bfloat16 [64, 2048, 768], P('expert', None, 'replica')
- grad_down: bfloat16 [64, 768, 2048], P('expert', 'replica')
The draws below stay inside these ranges and needn't reach their ends.
Inputs may be any that keep to these rules, and one draw needn't show every extreme that they name: `expert_ids`: each row names 8 different experts. Among the rows of one device at most 20 name the same expert, and in every draw some expert is named by exactly 20 rows of some device.
All inputs are finite; a program needn't handle non-finite values.
Results may differ from the reference program's by a relative error of at most 0.012.
Values may be sent and summed in bfloat16 or wider, within the bound.
No kernel may reach another device: no remote copies, remote signals or barrier semaphores. Data moves between devices by JAX's collectives and lax.ppermute only.
A program may use at most 192 MiB of HBM per device.

```python
import math
import jax
import jax.numpy as jnp
import numpy as np
from jax import lax

D = 2048
FF = 768
TOPK = 8
BLK = 128
TOK_DEV = 128
EXPERTS = 64
CAP = 20
TOKENS = 16384


def plant(result, stream_key, low, high):
    dims = result.shape
    index_at = [jax.random.randint(jax.random.fold_in(stream_key, axis), (), 0, dims[axis]) for axis in range(len(dims))]
    result = result.at[tuple(index_at)].set(low)
    longest = dims.index(max(dims))
    index_at[longest] = (index_at[longest] + 1) % dims[longest]
    return result.at[tuple(index_at)].set(high)


def steps_of(key, dims, cuts, least, top_value):
    loudness = 1.0
    for position, blocks in cuts:
        draws = jax.random.uniform(jax.random.fold_in(jax.random.fold_in(key, 6), position), (blocks,), jnp.float32, least / len(cuts), top_value / len(cuts))
        loudness = loudness * jnp.repeat(jnp.exp(draws), dims[position] // blocks).reshape((-1,) + (1,) * (len(dims) - 1 - position))
    return loudness


def assign_block(key, own, number, rows, number_of, top, bound, lean):
    order = jax.random.permutation(key, number_of)
    crowded, ordinary = portions_of(number_of, rows * top, bound, lean, True), portions_of(number_of, rows * top, bound, lean, False)
    places = jnp.arange(number_of)

    def named(tallies, turn):
        used = int((tallies > 0).sum())
        fixed = max(1, used // 4)
        passed = fixed + (places - fixed + turn * (used - fixed)) % max(1, number_of - fixed)
        return jnp.zeros((number_of,), jnp.int32).at[order[jnp.where(places < fixed, places, passed)]].set(jnp.asarray(tallies, jnp.int32))

    tallies = jnp.where(number % 4 == 0, named(crowded, number // 4), named(ordinary, number - number // 4 - 1))
    mixed = jax.random.permutation(jax.random.fold_in(own, 3), number_of)
    donor, taker = mixed[0:number_of // 2 * 2:2], mixed[1:number_of // 2 * 2:2]
    margin = jnp.minimum(tallies[donor] - 1, bound - tallies[taker]) // 2
    margin = jnp.where((donor == order[0]) | (taker == order[0]) | (tallies[taker] == 0), 0, jnp.maximum(margin, 0))
    passed = jax.random.randint(jax.random.fold_in(own, 4), (number_of // 2,), 0, 1 << 20) % (margin + 1)
    tallies = tallies.at[donor].add(-passed).at[taker].add(passed)
    items = jnp.searchsorted(jnp.cumsum(tallies), jnp.arange(rows * top), side="right").astype(jnp.int32)
    table = items.reshape(top, rows).T
    table = table[jax.random.permutation(jax.random.fold_in(own, 1), rows)]
    turn = jax.random.randint(jax.random.fold_in(own, 2), (rows, 1), 0, top)
    return jnp.take_along_axis(table, (jnp.arange(top)[None, :] + turn) % top, axis=1)


def portions_of(amount, total, most, lean, full):
    weights = [(1 << 20) // math.isqrt(rank ** lean) + 1 for rank in range(1, amount + 1)]
    largest = most if full else min(most, max(-(-total // amount), total * weights[0] // sum(weights)))
    least = 1 if total - largest >= amount - 1 else 0
    holding, surplus = [largest] + [least] * (amount - 1), total - largest - least * (amount - 1)
    while surplus > 0:
        movable = [i for i in range(1, amount) if holding[i] < largest] or [i for i in range(1, amount) if holding[i] < most]
        whole, budget = sum([weights[i] for i in movable]), surplus
        for i in movable:
            more = min(most - holding[i], max(1, budget * weights[i] // whole), surplus)
            holding[i] = holding[i] + more
            surplus = surplus - more
    return np.array(holding)


def noise(stream_key, extent, width, bound, split=(), kind=jnp.bfloat16):
    entries = jax.random.normal(stream_key, extent, jnp.float32) * width
    if len(split) > 0:
        entries = steps_of(stream_key, extent, split, -0.22, 0.18) * entries
    return jnp.clip(entries, min=-bound, max=bound).astype(kind)


def setup_inputs(seed: int = 0) -> dict:
    keys = jax.random.split(jax.random.key(seed), 12)
    x_quant = noise(keys[0], (TOKENS, D), 1.0, 6.0, ((0, 128),))
    x_scale = jnp.clip(jnp.exp(math.log(3.0) - 2.3025851 * jax.random.uniform(keys[1], (TOKENS, D // BLK), jnp.float32) ** steps_of(keys[1], (TOKENS, D // BLK), ((0, 128),), -0.2, 0.2)), 0.3, 3.0)
    out_grad = noise(keys[2], (TOKENS, D), 1.0, 6.0, ((0, 128),))
    expert_ids_keys = jax.random.split(jax.random.fold_in(keys[3], 1), TOKENS // TOK_DEV)
    expert_ids_turns = jax.random.permutation(jax.random.fold_in(keys[3], 3), TOKENS // TOK_DEV)
    expert_ids = jax.vmap(lambda own, number: assign_block(jax.random.fold_in(keys[3], 2), own, number, TOK_DEV, EXPERTS, TOPK, CAP, 2))(expert_ids_keys, expert_ids_turns).reshape((TOKENS, TOPK))
    gate_fixed = plant(jax.random.randint(keys[4], (TOKENS, TOPK), 1024, 16384), jax.random.fold_in(keys[4], 1), 1024, 16383).astype(jnp.int32)
    w_gate = noise(keys[5], (EXPERTS, D, FF), D ** -0.5, 0.125, ((0, 64),))
    s_gate = jnp.clip(jnp.exp(math.log(3.0) - 2.3025851 * jax.random.uniform(keys[6], (EXPERTS, D // BLK, FF // BLK), jnp.float32) ** steps_of(keys[6], (EXPERTS, D // BLK, FF // BLK), ((0, 64),), -0.2, 0.2)), 0.3, 3.0)
    w_up = noise(keys[7], (EXPERTS, D, FF), D ** -0.5, 0.125, ((0, 64),))
    s_up = jnp.clip(jnp.exp(math.log(3.0) - 2.3025851 * jax.random.uniform(keys[8], (EXPERTS, D // BLK, FF // BLK), jnp.float32) ** steps_of(keys[8], (EXPERTS, D // BLK, FF // BLK), ((0, 64),), -0.2, 0.2)), 0.3, 3.0)
    w_down = noise(keys[9], (EXPERTS, FF, D), FF ** -0.5, 0.21875, ((0, 64),))
    s_down = jnp.clip(jnp.exp(math.log(3.0) - 2.3025851 * jax.random.uniform(keys[10], (EXPERTS, FF // BLK, D // BLK), jnp.float32) ** steps_of(keys[10], (EXPERTS, FF // BLK, D // BLK), ((0, 64),), -0.2, 0.2)), 0.3, 3.0)
    return {"x_quant": x_quant, "x_scale": x_scale, "out_grad": out_grad, "expert_ids": expert_ids, "gate_fixed": gate_fixed, "w_gate": w_gate, "s_gate": s_gate, "w_up": w_up, "s_up": s_up, "w_down": w_down, "s_down": s_down}


def dequant(weight, scale):
    rows, cols = weight.shape
    srows, scols = scale.shape
    blocks = weight.reshape(srows, rows // srows, scols, cols // scols).astype(jnp.float32)
    return (blocks * scale[:, None, :, None]).reshape(rows, cols).astype(jnp.bfloat16)


def block_slots(flat_ids):
    onehot = (flat_ids[:, None] == jnp.arange(EXPERTS, dtype=jnp.int32)[None, :]).astype(jnp.int32)
    before = jnp.cumsum(onehot, axis=0) - onehot
    return jnp.sum(before * onehot, axis=1).astype(jnp.int32)


def reference(x_quant, x_scale, out_grad, expert_ids, gate_fixed, w_gate, s_gate, w_up, s_up, w_down, s_down):
    blocks_count = TOKENS // TOK_DEV
    scaled = x_quant.reshape(TOKENS, D // BLK, BLK).astype(jnp.float32) * x_scale[:, :, None]
    inputs = scaled.reshape(TOKENS, D).astype(jnp.bfloat16)
    flat = expert_ids.reshape(blocks_count, TOK_DEV * TOPK).astype(jnp.int32)
    slots = jax.vmap(block_slots)(flat)
    within = (jnp.arange(TOK_DEV * TOPK, dtype=jnp.int32) // TOPK)[None, :]
    owners = jnp.arange(blocks_count, dtype=jnp.int32)[:, None]
    token_index = (owners * TOK_DEV + within).astype(jnp.int32)
    owner_full = jnp.broadcast_to(owners, flat.shape)
    table = jnp.full((EXPERTS, blocks_count, CAP), TOKENS, jnp.int32).at[flat, owner_full, slots].set(token_index)
    gate_vals = gate_fixed.reshape(blocks_count, TOK_DEV * TOPK).astype(jnp.float32) / 65536.0
    gate_table = jnp.zeros((EXPERTS, blocks_count, CAP), jnp.float32).at[flat, owner_full, slots].set(gate_vals)
    input_pad = jnp.concatenate([inputs, jnp.zeros((1, D), jnp.bfloat16)], axis=0)
    grad_pad = jnp.concatenate([out_grad, jnp.zeros((1, D), jnp.bfloat16)], axis=0)

    def one_expert(total, packed):
        index, gates, wg, sg, wu, su, wd, sd = packed
        rows = index.reshape(-1)
        gate_w = dequant(wg, sg)
        up_w = dequant(wu, su)
        down_w = dequant(wd, sd)
        xrows = input_pad[rows]
        row_grad = (gates.reshape(-1)[:, None] * grad_pad[rows].astype(jnp.float32)).astype(jnp.bfloat16)
        pre_gate = jnp.dot(xrows, gate_w, preferred_element_type=jnp.float32)
        pre_up = jnp.dot(xrows, up_w, preferred_element_type=jnp.float32)
        sig = jax.nn.sigmoid(pre_gate)
        act = pre_gate * sig
        hidden = (act * pre_up).astype(jnp.bfloat16)
        hidden_grad = jnp.dot(row_grad, down_w.T, preferred_element_type=jnp.float32)
        up_grad = (hidden_grad * act).astype(jnp.bfloat16)
        gate_grad = (hidden_grad * pre_up * sig * (1.0 + pre_gate * (1.0 - sig))).astype(jnp.bfloat16)
        row_input = jnp.dot(gate_grad, gate_w.T, preferred_element_type=jnp.float32)
        row_input = row_input + jnp.dot(up_grad, up_w.T, preferred_element_type=jnp.float32)
        row_input = lax.optimization_barrier(row_input.astype(jnp.bfloat16)).astype(jnp.float32)
        total = total.at[rows].add(row_input)
        grad_g = jnp.dot(xrows.T, gate_grad, preferred_element_type=jnp.float32).astype(jnp.bfloat16)
        grad_u = jnp.dot(xrows.T, up_grad, preferred_element_type=jnp.float32).astype(jnp.bfloat16)
        grad_d = jnp.dot(hidden.T, row_grad, preferred_element_type=jnp.float32).astype(jnp.bfloat16)
        return total, (grad_g, grad_u, grad_d)

    start = jnp.zeros((TOKENS + 1, D), jnp.float32)
    total, (grad_gate, grad_up, grad_down) = lax.scan(one_expert, start, (table, gate_table, w_gate, s_gate, w_up, s_up, w_down, s_down))
    return total[:TOKENS].astype(jnp.bfloat16), grad_gate, grad_up, grad_down
```

```python
import jax
import jax.numpy as jnp
from jax import lax
from jax.sharding import PartitionSpec as P

LANES = 128


def dequant(weight, scale):
    rows, cols = weight.shape
    srows, scols = scale.shape
    blocks = weight.reshape(srows, rows // srows, scols, cols // scols).astype(jnp.float32)
    return (blocks * scale[:, None, :, None]).reshape(rows, cols).astype(jnp.bfloat16)


def forward_parts(xrows, gate_w, up_w):
    pre_gate = jnp.dot(xrows, gate_w, preferred_element_type=jnp.float32)
    pre_up = jnp.dot(xrows, up_w, preferred_element_type=jnp.float32)
    sig = jax.nn.sigmoid(pre_gate)
    act = pre_gate * sig
    return (pre_gate, pre_up, sig, act)


def unit_grads(row_grad, down_w, pre_gate, pre_up, sig, act):
    hidden_grad = jnp.dot(row_grad, down_w.T, preferred_element_type=jnp.float32)
    up_grad = (hidden_grad * act).astype(jnp.bfloat16)
    gate_grad = (hidden_grad * pre_up * sig * (1.0 + pre_gate * (1.0 - sig))).astype(jnp.bfloat16)
    return (gate_grad, up_grad)


def routing(expert_ids, gate_fixed, experts, capacity):
    tok_rows, topk = expert_ids.shape
    n = tok_rows * topk
    flat_ids = expert_ids.reshape(-1)
    onehot = flat_ids[:, None] == jnp.arange(experts, dtype=jnp.int32)[None, :]
    order = jnp.arange(n, dtype=jnp.int32)
    lower = (order[None, :] < order[:, None]).astype(jnp.bfloat16)
    before = jnp.dot(lower, onehot.astype(jnp.bfloat16), preferred_element_type=jnp.float32)
    slot_of = jnp.sum(jnp.where(onehot, before, 0.0), axis=1).astype(jnp.int32)
    dest = flat_ids * capacity + slot_of
    places = jnp.arange(experts * capacity, dtype=jnp.int32)
    pick = (dest[None, :] == places[:, None]).astype(jnp.bfloat16)
    flat_gate = gate_fixed.reshape(-1)
    token_of = order // topk
    cols = jnp.stack(
        [token_of, jnp.ones_like(token_of), flat_gate // 128, flat_gate % 128], axis=1
    ).astype(jnp.bfloat16)
    got = jnp.dot(pick, cols, preferred_element_type=jnp.float32)
    used = got[:, 1] > 0.5
    table = jnp.where(used, got[:, 0], float(tok_rows)).astype(jnp.int32)
    gate_table = (got[:, 2] * 128.0 + got[:, 3]) / 65536.0
    return dest, table, gate_table


def shards(
    x_quant, x_scale, out_grad, expert_ids, gate_fixed, w_gate, s_gate, w_up, s_up, w_down, s_down
):
    tok_rows, width = x_quant.shape
    topk = expert_ids.shape[1]
    experts = lax.axis_size("expert")
    capacity = tok_rows * topk * 5 // (4 * experts)
    sub = width // LANES
    blk_width = width // x_scale.shape[1]
    dest, table, gate_table = routing(expert_ids, gate_fixed, experts, capacity)
    scaled = x_quant.reshape(tok_rows, -1, blk_width).astype(jnp.float32) * x_scale[:, :, None]
    inputs = scaled.reshape(tok_rows, sub, LANES).astype(jnp.bfloat16)
    zero_row = jnp.zeros((1, sub, LANES), jnp.bfloat16)
    input_pad = jnp.concatenate([inputs, zero_row], axis=0)
    grad_pad = jnp.concatenate([out_grad.reshape(tok_rows, sub, LANES), zero_row], axis=0)
    send_rows = input_pad[table]
    send_grads = (gate_table[:, None, None] * grad_pad[table].astype(jnp.float32)).astype(jnp.bfloat16)
    payload = jnp.concatenate(
        [
            send_rows.reshape(experts, capacity * sub, LANES),
            send_grads.reshape(experts, capacity * sub, LANES),
        ],
        axis=1,
    )
    got = lax.all_to_all(payload, "expert", split_axis=0, concat_axis=0, tiled=True)
    rows_in = experts * capacity
    xrows = got[:, : capacity * sub].reshape(rows_in, width)
    row_grad = got[:, capacity * sub :].reshape(rows_in, width)
    gate_w = dequant(w_gate[0], s_gate[0])
    up_w = dequant(w_up[0], s_up[0])
    down_w = dequant(w_down[0], s_down[0])
    pre_gate, pre_up, sig, act = forward_parts(xrows, gate_w, up_w)
    hidden = (act * pre_up).astype(jnp.bfloat16)
    gate_grad, up_grad = unit_grads(row_grad, down_w, pre_gate, pre_up, sig, act)
    row_input = jnp.dot(gate_grad, gate_w.T, preferred_element_type=jnp.float32)
    row_input = row_input + jnp.dot(up_grad, up_w.T, preferred_element_type=jnp.float32)
    back_rows = row_input.astype(jnp.bfloat16).reshape(experts, capacity * sub, LANES)
    returned = lax.all_to_all(back_rows, "expert", split_axis=0, concat_axis=0, tiled=True)
    term_gate = jnp.dot(xrows.T, gate_grad, preferred_element_type=jnp.float32)
    term_up = jnp.dot(xrows.T, up_grad, preferred_element_type=jnp.float32)
    term_down = jnp.dot(hidden.T, row_grad, preferred_element_type=jnp.float32)
    sum_gate, sum_up, sum_down = (
        lax.psum_scatter(
            term_gate.astype(jnp.bfloat16), "replica", scatter_dimension=1, tiled=True
        ).astype(jnp.float32),
        lax.psum_scatter(
            term_up.astype(jnp.bfloat16), "replica", scatter_dimension=1, tiled=True
        ).astype(jnp.float32),
        lax.psum_scatter(
            term_down.astype(jnp.bfloat16), "replica", scatter_dimension=0, tiled=True
        ).astype(jnp.float32),
    )
    picked = returned.reshape(rows_in, sub, LANES)[dest].astype(jnp.float32)
    grad_input = jnp.sum(picked.reshape(tok_rows, topk, sub, LANES), axis=1)
    grad_input = grad_input.reshape(tok_rows, width).astype(jnp.bfloat16)
    grad_gate = sum_gate.astype(jnp.bfloat16)[None]
    grad_up = sum_up.astype(jnp.bfloat16)[None]
    grad_down = sum_down.astype(jnp.bfloat16)[None]
    return (grad_input, grad_gate, grad_up, grad_down)


def solution(mesh):
    placed = (
        P(("expert", "replica"), None),
        P(("expert", "replica"), None),
        P(("expert", "replica"), None),
        P(("expert", "replica"), None),
        P(("expert", "replica"), None),
        P("expert", None, None),
        P("expert", None, None),
        P("expert", None, None),
        P("expert", None, None),
        P("expert", None, None),
        P("expert", None, None),
    )
    return jax.shard_map(
        shards,
        mesh=mesh,
        in_specs=placed,
        out_specs=(
            P(("expert", "replica"), None),
            P("expert", None, "replica"),
            P("expert", None, "replica"),
            P("expert", "replica", None),
        ),
        check_vma=False,
    )
```

```python
import jax
import jax.numpy as jnp
from jax import lax
from jax.sharding import PartitionSpec as P

LANES = 128
CHUNKS = 4


def dequant(weight, scale):
    rows, cols = weight.shape
    srows, scols = scale.shape
    blocks = weight.reshape(srows, rows // srows, scols, cols // scols).astype(jnp.float32)
    return (blocks * scale[:, None, :, None]).reshape(rows, cols).astype(jnp.bfloat16)


def forward_parts(xrows, gate_w, up_w):
    pre_gate = jnp.dot(xrows, gate_w, preferred_element_type=jnp.float32)
    pre_up = jnp.dot(xrows, up_w, preferred_element_type=jnp.float32)
    sig = jax.nn.sigmoid(pre_gate)
    act = pre_gate * sig
    return (pre_gate, pre_up, sig, act)


def unit_grads(row_grad, down_w, pre_gate, pre_up, sig, act):
    hidden_grad = jnp.dot(row_grad, down_w.T, preferred_element_type=jnp.float32)
    up_grad = (hidden_grad * act).astype(jnp.bfloat16)
    gate_grad = (hidden_grad * pre_up * sig * (1.0 + pre_gate * (1.0 - sig))).astype(jnp.bfloat16)
    return (gate_grad, up_grad)


def routing(expert_ids, gate_fixed, experts, capacity):
    tok_rows, topk = expert_ids.shape
    n = tok_rows * topk
    flat_ids = expert_ids.reshape(-1)
    onehot = flat_ids[:, None] == jnp.arange(experts, dtype=jnp.int32)[None, :]
    order = jnp.arange(n, dtype=jnp.int32)
    lower = (order[None, :] < order[:, None]).astype(jnp.bfloat16)
    before = jnp.dot(lower, onehot.astype(jnp.bfloat16), preferred_element_type=jnp.float32)
    slot_of = jnp.sum(jnp.where(onehot, before, 0.0), axis=1).astype(jnp.int32)
    dest = flat_ids * capacity + slot_of
    places = jnp.arange(experts * capacity, dtype=jnp.int32)
    pick = (dest[None, :] == places[:, None]).astype(jnp.bfloat16)
    flat_gate = gate_fixed.reshape(-1)
    token_of = order // topk
    cols = jnp.stack(
        [token_of, jnp.ones_like(token_of), flat_gate // 128, flat_gate % 128], axis=1
    ).astype(jnp.bfloat16)
    got = jnp.dot(pick, cols, preferred_element_type=jnp.float32)
    used = got[:, 1] > 0.5
    table = jnp.where(used, got[:, 0], float(tok_rows)).astype(jnp.int32)
    gate_table = (got[:, 2] * 128.0 + got[:, 3]) / 65536.0
    return dest, table, gate_table


def shards(
    x_quant, x_scale, out_grad, expert_ids, gate_fixed, w_gate, s_gate, w_up, s_up, w_down, s_down
):
    tok_rows, width = x_quant.shape
    topk = expert_ids.shape[1]
    experts = lax.axis_size("expert")
    capacity = tok_rows * topk * 5 // (4 * experts)
    chunks = CHUNKS if capacity % CHUNKS == 0 else 1
    per = capacity // chunks
    sub = width // LANES
    blk_width = width // x_scale.shape[1]
    dest, table, gate_table = routing(expert_ids, gate_fixed, experts, capacity)
    scaled = x_quant.reshape(tok_rows, -1, blk_width).astype(jnp.float32) * x_scale[:, :, None]
    inputs = scaled.reshape(tok_rows, sub, LANES).astype(jnp.bfloat16)
    zero_row = jnp.zeros((1, sub, LANES), jnp.bfloat16)
    input_pad = jnp.concatenate([inputs, zero_row], axis=0)
    grad_pad = jnp.concatenate([out_grad.reshape(tok_rows, sub, LANES), zero_row], axis=0)
    table = table.reshape(experts, capacity)
    gate_table = gate_table.reshape(experts, capacity)
    gate_w = dequant(w_gate[0], s_gate[0])
    up_w = dequant(w_up[0], s_up[0])
    down_w = dequant(w_down[0], s_down[0])
    rows_in = experts * per
    span = per * sub

    def payload_of(c):
        idx = table[:, c * per : (c + 1) * per]
        gates = gate_table[:, c * per : (c + 1) * per]
        send_rows = input_pad[idx]
        send_grads = (gates[:, :, None, None] * grad_pad[idx].astype(jnp.float32)).astype(jnp.bfloat16)
        return [send_rows.reshape(experts, span, LANES), send_grads.reshape(experts, span, LANES)]

    def compute(got):
        xrows = got[:, :span].reshape(rows_in, width)
        row_grad = got[:, span : 2 * span].reshape(rows_in, width)
        pre_gate, pre_up, sig, act = forward_parts(xrows, gate_w, up_w)
        hidden = (act * pre_up).astype(jnp.bfloat16)
        gate_grad, up_grad = unit_grads(row_grad, down_w, pre_gate, pre_up, sig, act)
        row_input = jnp.dot(gate_grad, gate_w.T, preferred_element_type=jnp.float32)
        row_input = row_input + jnp.dot(up_grad, up_w.T, preferred_element_type=jnp.float32)
        back_rows = row_input.astype(jnp.bfloat16).reshape(experts, span, LANES)
        part_gate = jnp.dot(xrows.T, gate_grad, preferred_element_type=jnp.float32)
        part_up = jnp.dot(xrows.T, up_grad, preferred_element_type=jnp.float32)
        part_down = jnp.dot(hidden.T, row_grad, preferred_element_type=jnp.float32)
        return back_rows, (part_gate, part_up, part_down)

    terms = None
    arrived = [None] * chunks
    backs = [None] * chunks
    returned = [None] * chunks
    for step in range(chunks + 2):
        pieces = []
        if step < chunks:
            pieces += payload_of(step)
        if step >= 2:
            pieces.append(backs[step - 2])
        got = lax.all_to_all(
            jnp.concatenate(pieces, axis=1), "expert", split_axis=0, concat_axis=0, tiled=True
        )
        if step < chunks:
            arrived[step] = got
        if step >= 2:
            returned[step - 2] = got[:, -span:]
        if 1 <= step <= chunks:
            backs[step - 1], parts = compute(arrived[step - 1])
            terms = parts if terms is None else tuple(a + b for a, b in zip(terms, parts))
    term_gate, term_up, term_down = terms
    sum_gate, sum_up, sum_down = (
        lax.psum_scatter(
            term_gate.astype(jnp.bfloat16), "replica", scatter_dimension=1, tiled=True
        ).astype(jnp.float32),
        lax.psum_scatter(
            term_up.astype(jnp.bfloat16), "replica", scatter_dimension=1, tiled=True
        ).astype(jnp.float32),
        lax.psum_scatter(
            term_down.astype(jnp.bfloat16), "replica", scatter_dimension=0, tiled=True
        ).astype(jnp.float32),
    )
    back = jnp.concatenate(
        [r.reshape(experts, per, sub, LANES) for r in returned], axis=1
    ).reshape(experts * capacity, sub, LANES)
    picked = back[dest].astype(jnp.float32)
    grad_input = jnp.sum(picked.reshape(tok_rows, topk, sub, LANES), axis=1)
    grad_input = grad_input.reshape(tok_rows, width).astype(jnp.bfloat16)
    grad_gate = sum_gate.astype(jnp.bfloat16)[None]
    grad_up = sum_up.astype(jnp.bfloat16)[None]
    grad_down = sum_down.astype(jnp.bfloat16)[None]
    return (grad_input, grad_gate, grad_up, grad_down)


def solution(mesh):
    placed = (
        P(("expert", "replica"), None),
        P(("expert", "replica"), None),
        P(("expert", "replica"), None),
        P(("expert", "replica"), None),
        P(("expert", "replica"), None),
        P("expert", None, None),
        P("expert", None, None),
        P("expert", None, None),
        P("expert", None, None),
        P("expert", None, None),
        P("expert", None, None),
    )
    return jax.shard_map(
        shards,
        mesh=mesh,
        in_specs=placed,
        out_specs=(
            P(("expert", "replica"), None),
            P("expert", None, "replica"),
            P("expert", None, "replica"),
            P("expert", "replica", None),
        ),
        check_vma=False,
    )
```

```python
import jax
import jax.numpy as jnp
from jax import lax
from jax.sharding import PartitionSpec as P

LANES = 128
CHUNKS = 4


def dequant(weight, scale):
    rows, cols = weight.shape
    srows, scols = scale.shape
    blocks = weight.reshape(srows, rows // srows, scols, cols // scols).astype(jnp.float32)
    return (blocks * scale[:, None, :, None]).reshape(rows, cols).astype(jnp.bfloat16)


def forward_parts(xrows, gate_w, up_w):
    pre_gate = jnp.dot(xrows, gate_w, preferred_element_type=jnp.float32)
    pre_up = jnp.dot(xrows, up_w, preferred_element_type=jnp.float32)
    sig = jax.nn.sigmoid(pre_gate)
    act = pre_gate * sig
    return (pre_gate, pre_up, sig, act)


def unit_grads(row_grad, down_w, pre_gate, pre_up, sig, act):
    hidden_grad = jnp.dot(row_grad, down_w.T, preferred_element_type=jnp.float32)
    up_grad = (hidden_grad * act).astype(jnp.bfloat16)
    gate_grad = (hidden_grad * pre_up * sig * (1.0 + pre_gate * (1.0 - sig))).astype(jnp.bfloat16)
    return (gate_grad, up_grad)


def routing(expert_ids, gate_fixed, experts, capacity):
    tok_rows, topk = expert_ids.shape
    n = tok_rows * topk
    flat_ids = expert_ids.reshape(-1)
    onehot = flat_ids[:, None] == jnp.arange(experts, dtype=jnp.int32)[None, :]
    order = jnp.arange(n, dtype=jnp.int32)
    lower = (order[None, :] < order[:, None]).astype(jnp.bfloat16)
    before = jnp.dot(lower, onehot.astype(jnp.bfloat16), preferred_element_type=jnp.float32)
    slot_of = jnp.sum(jnp.where(onehot, before, 0.0), axis=1).astype(jnp.int32)
    dest = flat_ids * capacity + slot_of
    places = jnp.arange(experts * capacity, dtype=jnp.int32)
    pick = (dest[None, :] == places[:, None]).astype(jnp.bfloat16)
    flat_gate = gate_fixed.reshape(-1)
    token_of = order // topk
    cols = jnp.stack(
        [token_of, jnp.ones_like(token_of), flat_gate // 128, flat_gate % 128], axis=1
    ).astype(jnp.bfloat16)
    got = jnp.dot(pick, cols, preferred_element_type=jnp.float32)
    used = got[:, 1] > 0.5
    table = jnp.where(used, got[:, 0], float(tok_rows)).astype(jnp.int32)
    gate_table = (got[:, 2] * 128.0 + got[:, 3]) / 65536.0
    return dest, table, gate_table


def shards(
    x_quant, x_scale, out_grad, expert_ids, gate_fixed, w_gate, s_gate, w_up, s_up, w_down, s_down
):
    tok_rows, width = x_quant.shape
    topk = expert_ids.shape[1]
    experts = lax.axis_size("expert")
    capacity = tok_rows * topk * 5 // (4 * experts)
    chunks = CHUNKS if capacity % CHUNKS == 0 else 1
    per = capacity // chunks
    sub = width // LANES
    blk_width = width // x_scale.shape[1]
    dest, table, gate_table = routing(expert_ids, gate_fixed, experts, capacity)
    scaled = x_quant.reshape(tok_rows, -1, blk_width).astype(jnp.float32) * x_scale[:, :, None]
    inputs = scaled.reshape(tok_rows, sub, LANES).astype(jnp.bfloat16)
    zero_row = jnp.zeros((1, sub, LANES), jnp.bfloat16)
    input_pad = jnp.concatenate([inputs, zero_row], axis=0)
    grad_pad = jnp.concatenate([out_grad.reshape(tok_rows, sub, LANES), zero_row], axis=0)
    table = table.reshape(experts, capacity)
    gate_table = gate_table.reshape(experts, capacity)
    gate_w = dequant(w_gate[0], s_gate[0])
    up_w = dequant(w_up[0], s_up[0])
    down_w = dequant(w_down[0], s_down[0])
    rows_in = experts * per
    span = per * sub

    def payload_of(c):
        idx = table[:, c * per : (c + 1) * per]
        gates = gate_table[:, c * per : (c + 1) * per]
        send_rows = input_pad[idx]
        send_grads = (gates[:, :, None, None] * grad_pad[idx].astype(jnp.float32)).astype(jnp.bfloat16)
        return [send_rows.reshape(experts, span, LANES), send_grads.reshape(experts, span, LANES)]

    def compute(got):
        xrows = got[:, :span].reshape(rows_in, width)
        row_grad = got[:, span : 2 * span].reshape(rows_in, width)
        pre_gate, pre_up, sig, act = forward_parts(xrows, gate_w, up_w)
        hidden = (act * pre_up).astype(jnp.bfloat16)
        gate_grad, up_grad = unit_grads(row_grad, down_w, pre_gate, pre_up, sig, act)
        row_input = jnp.dot(gate_grad, gate_w.T, preferred_element_type=jnp.float32)
        row_input = row_input + jnp.dot(up_grad, up_w.T, preferred_element_type=jnp.float32)
        back_rows = row_input.astype(jnp.bfloat16).reshape(experts, span, LANES)
        return back_rows, (xrows, row_grad, hidden, gate_grad, up_grad)

    saved = []
    arrived = [None] * chunks
    backs = [None] * chunks
    returned = [None] * chunks
    for step in range(chunks + 2):
        pieces = []
        if step < chunks:
            pieces += payload_of(step)
        if step >= 2:
            pieces.append(backs[step - 2])
        got = lax.all_to_all(
            jnp.concatenate(pieces, axis=1), "expert", split_axis=0, concat_axis=0, tiled=True
        )
        if step < chunks:
            arrived[step] = got
        if step >= 2:
            returned[step - 2] = got[:, -span:]
        if 1 <= step <= chunks:
            backs[step - 1], kept = compute(arrived[step - 1])
            saved.append(kept)
    xrows, row_grad, hidden, gate_grad, up_grad = (
        jnp.concatenate(list(group), axis=0) for group in zip(*saved)
    )
    term_gate = jnp.dot(xrows.T, gate_grad, preferred_element_type=jnp.float32)
    term_up = jnp.dot(xrows.T, up_grad, preferred_element_type=jnp.float32)
    term_down = jnp.dot(hidden.T, row_grad, preferred_element_type=jnp.float32)
    sum_gate, sum_up, sum_down = (
        lax.psum_scatter(
            term_gate.astype(jnp.bfloat16), "replica", scatter_dimension=1, tiled=True
        ).astype(jnp.float32),
        lax.psum_scatter(
            term_up.astype(jnp.bfloat16), "replica", scatter_dimension=1, tiled=True
        ).astype(jnp.float32),
        lax.psum_scatter(
            term_down.astype(jnp.bfloat16), "replica", scatter_dimension=0, tiled=True
        ).astype(jnp.float32),
    )
    back = jnp.concatenate(
        [r.reshape(experts, per, sub, LANES) for r in returned], axis=1
    ).reshape(experts * capacity, sub, LANES)
    picked = back[dest].astype(jnp.float32)
    grad_input = jnp.sum(picked.reshape(tok_rows, topk, sub, LANES), axis=1)
    grad_input = grad_input.reshape(tok_rows, width).astype(jnp.bfloat16)
    grad_gate = sum_gate.astype(jnp.bfloat16)[None]
    grad_up = sum_up.astype(jnp.bfloat16)[None]
    grad_down = sum_down.astype(jnp.bfloat16)[None]
    return (grad_input, grad_gate, grad_up, grad_down)


def solution(mesh):
    placed = (
        P(("expert", "replica"), None),
        P(("expert", "replica"), None),
        P(("expert", "replica"), None),
        P(("expert", "replica"), None),
        P(("expert", "replica"), None),
        P("expert", None, None),
        P("expert", None, None),
        P("expert", None, None),
        P("expert", None, None),
        P("expert", None, None),
        P("expert", None, None),
    )
    return jax.shard_map(
        shards,
        mesh=mesh,
        in_specs=placed,
        out_specs=(
            P(("expert", "replica"), None),
            P("expert", None, "replica"),
            P("expert", None, "replica"),
            P("expert", "replica", None),
        ),
        check_vma=False,
    )
```

```python
import jax
import jax.numpy as jnp
from jax import lax
from jax.sharding import PartitionSpec as P

LANES = 128
CHUNKS = 4


def dequant(weight, scale):
    rows, cols = weight.shape
    srows, scols = scale.shape
    blocks = weight.reshape(srows, rows // srows, scols, cols // scols).astype(jnp.float32)
    return (blocks * scale[:, None, :, None]).reshape(rows, cols).astype(jnp.bfloat16)


def forward_parts(xrows, gate_w, up_w):
    pre_gate = jnp.dot(xrows, gate_w, preferred_element_type=jnp.float32)
    pre_up = jnp.dot(xrows, up_w, preferred_element_type=jnp.float32)
    sig = jax.nn.sigmoid(pre_gate)
    act = pre_gate * sig
    return (pre_gate, pre_up, sig, act)


def unit_grads(row_grad, down_w, pre_gate, pre_up, sig, act):
    hidden_grad = jnp.dot(row_grad, down_w.T, preferred_element_type=jnp.float32)
    up_grad = (hidden_grad * act).astype(jnp.bfloat16)
    gate_grad = (hidden_grad * pre_up * sig * (1.0 + pre_gate * (1.0 - sig))).astype(jnp.bfloat16)
    return (gate_grad, up_grad)


def routing(expert_ids, gate_fixed, experts, capacity):
    tok_rows, topk = expert_ids.shape
    n = tok_rows * topk
    flat_ids = expert_ids.reshape(-1)
    onehot = flat_ids[:, None] == jnp.arange(experts, dtype=jnp.int32)[None, :]
    order = jnp.arange(n, dtype=jnp.int32)
    lower = (order[None, :] < order[:, None]).astype(jnp.bfloat16)
    before = jnp.dot(lower, onehot.astype(jnp.bfloat16), preferred_element_type=jnp.float32)
    slot_of = jnp.sum(jnp.where(onehot, before, 0.0), axis=1).astype(jnp.int32)
    dest = flat_ids * capacity + slot_of
    places = jnp.arange(experts * capacity, dtype=jnp.int32)
    pick = (dest[None, :] == places[:, None]).astype(jnp.bfloat16)
    flat_gate = gate_fixed.reshape(-1)
    token_of = order // topk
    cols = jnp.stack(
        [token_of, jnp.ones_like(token_of), flat_gate // 128, flat_gate % 128], axis=1
    ).astype(jnp.bfloat16)
    got = jnp.dot(pick, cols, preferred_element_type=jnp.float32)
    used = got[:, 1] > 0.5
    table = jnp.where(used, got[:, 0], float(tok_rows)).astype(jnp.int32)
    gate_table = (got[:, 2] * 128.0 + got[:, 3]) / 65536.0
    return flat_ids, slot_of, table, gate_table


def shards(
    x_quant, x_scale, out_grad, expert_ids, gate_fixed, w_gate, s_gate, w_up, s_up, w_down, s_down
):
    tok_rows, width = x_quant.shape
    topk = expert_ids.shape[1]
    experts = lax.axis_size("expert")
    capacity = tok_rows * topk * 5 // (4 * experts)
    chunks = CHUNKS if capacity % CHUNKS == 0 else 1
    per = capacity // chunks
    sub = width // LANES
    blk_width = width // x_scale.shape[1]
    flat_ids, slot_of, table, gate_table = routing(expert_ids, gate_fixed, experts, capacity)
    scaled = x_quant.reshape(tok_rows, -1, blk_width).astype(jnp.float32) * x_scale[:, :, None]
    inputs = scaled.reshape(tok_rows, sub, LANES).astype(jnp.bfloat16)
    zero_row = jnp.zeros((1, sub, LANES), jnp.bfloat16)
    input_pad = jnp.concatenate([inputs, zero_row], axis=0)
    grad_pad = jnp.concatenate([out_grad.reshape(tok_rows, sub, LANES), zero_row], axis=0)
    table = table.reshape(experts, capacity)
    gate_table = gate_table.reshape(experts, capacity)
    gate_w = dequant(w_gate[0], s_gate[0])
    up_w = dequant(w_up[0], s_up[0])
    down_w = dequant(w_down[0], s_down[0])
    rows_in = experts * per
    span = per * sub

    def payload_of(c):
        idx = table[:, c * per : (c + 1) * per]
        gates = gate_table[:, c * per : (c + 1) * per]
        send_rows = input_pad[idx]
        send_grads = (gates[:, :, None, None] * grad_pad[idx].astype(jnp.float32)).astype(jnp.bfloat16)
        return [send_rows.reshape(experts, span, LANES), send_grads.reshape(experts, span, LANES)]

    def compute(got):
        xrows = got[:, :span].reshape(rows_in, width)
        row_grad = got[:, span : 2 * span].reshape(rows_in, width)
        pre_gate, pre_up, sig, act = forward_parts(xrows, gate_w, up_w)
        hidden = (act * pre_up).astype(jnp.bfloat16)
        gate_grad, up_grad = unit_grads(row_grad, down_w, pre_gate, pre_up, sig, act)
        row_input = jnp.dot(gate_grad, gate_w.T, preferred_element_type=jnp.float32)
        row_input = row_input + jnp.dot(up_grad, up_w.T, preferred_element_type=jnp.float32)
        back_rows = row_input.astype(jnp.bfloat16).reshape(experts, span, LANES)
        return back_rows, (xrows, row_grad, hidden, gate_grad, up_grad)

    saved = []
    arrived = [None] * chunks
    backs = [None] * chunks
    returned = [None] * chunks
    for step in range(chunks + 2):
        pieces = []
        if step < chunks:
            pieces += payload_of(step)
        if step >= 2:
            pieces.append(backs[step - 2])
        got = lax.all_to_all(
            jnp.concatenate(pieces, axis=1), "expert", split_axis=0, concat_axis=0, tiled=True
        )
        if step < chunks:
            arrived[step] = got
        if step >= 2:
            returned[step - 2] = got[:, -span:]
        if 1 <= step <= chunks:
            backs[step - 1], kept = compute(arrived[step - 1])
            saved.append(kept)
    xrows, row_grad, hidden, gate_grad, up_grad = (
        jnp.concatenate(list(group), axis=0) for group in zip(*saved)
    )
    ff = gate_grad.shape[1]
    half = ff // lax.axis_size("replica")
    mine = lax.axis_index("replica")
    other = 1 - mine

    def cols(a, r):
        return lax.dynamic_slice_in_dim(a, r * half, half, axis=1)

    def weight_parts(r):
        part_gate = jnp.dot(xrows.T, cols(gate_grad, r), preferred_element_type=jnp.float32)
        part_up = jnp.dot(xrows.T, cols(up_grad, r), preferred_element_type=jnp.float32)
        part_down = jnp.dot(cols(hidden, r).T, row_grad, preferred_element_type=jnp.float32)
        return tuple(p.astype(jnp.bfloat16) for p in (part_gate, part_up, part_down))

    sent = weight_parts(other)
    kept = weight_parts(mine)
    swap = [(0, 1), (1, 0)]
    came = tuple(lax.ppermute(p, "replica", swap) for p in sent)
    grad_gate, grad_up, grad_down = (
        (k.astype(jnp.float32) + c.astype(jnp.float32)).astype(jnp.bfloat16)[None]
        for k, c in zip(kept, came)
    )
    total = None
    for c in range(chunks):
        in_chunk = (slot_of // per) == c
        col = jnp.where(in_chunk, flat_ids * per + slot_of % per, -1)
        spots = jnp.arange(rows_in, dtype=jnp.int32)
        hit = (col[:, None] == spots[None, :]).astype(jnp.bfloat16)
        gather_mat = jnp.sum(hit.reshape(tok_rows, topk, rows_in), axis=1)
        back3 = returned[c].reshape(rows_in, sub, LANES)
        part = jnp.einsum("tj,jkl->tkl", gather_mat, back3, preferred_element_type=jnp.float32)
        total = part if total is None else total + part
    grad_input = total.reshape(tok_rows, width).astype(jnp.bfloat16)
    return (grad_input, grad_gate, grad_up, grad_down)


def solution(mesh):
    placed = (
        P(("expert", "replica"), None),
        P(("expert", "replica"), None),
        P(("expert", "replica"), None),
        P(("expert", "replica"), None),
        P(("expert", "replica"), None),
        P("expert", None, None),
        P("expert", None, None),
        P("expert", None, None),
        P("expert", None, None),
        P("expert", None, None),
        P("expert", None, None),
    )
    return jax.shard_map(
        shards,
        mesh=mesh,
        in_specs=placed,
        out_specs=(
            P(("expert", "replica"), None),
            P("expert", None, "replica"),
            P("expert", None, "replica"),
            P("expert", "replica", None),
        ),
        check_vma=False,
    )
```

```python
import jax
import jax.numpy as jnp
from jax import lax
from jax.sharding import PartitionSpec as P

LANES = 128
CHUNKS = 4


def dequant(weight, scale):
    rows, cols = weight.shape
    srows, scols = scale.shape
    blocks = weight.reshape(srows, rows // srows, scols, cols // scols).astype(jnp.float32)
    return (blocks * scale[:, None, :, None]).reshape(rows, cols).astype(jnp.bfloat16)


def forward_parts(xrows, gate_w, up_w):
    pre_gate = jnp.dot(xrows, gate_w, preferred_element_type=jnp.float32)
    pre_up = jnp.dot(xrows, up_w, preferred_element_type=jnp.float32)
    sig = jax.nn.sigmoid(pre_gate)
    act = pre_gate * sig
    return (pre_gate, pre_up, sig, act)


def unit_grads(row_grad, down_w, pre_gate, pre_up, sig, act):
    hidden_grad = jnp.dot(row_grad, down_w.T, preferred_element_type=jnp.float32)
    up_grad = (hidden_grad * act).astype(jnp.bfloat16)
    gate_grad = (hidden_grad * pre_up * sig * (1.0 + pre_gate * (1.0 - sig))).astype(jnp.bfloat16)
    return (gate_grad, up_grad)


def routing(expert_ids, gate_fixed, experts, capacity):
    tok_rows, topk = expert_ids.shape
    n = tok_rows * topk
    flat_ids = expert_ids.reshape(-1)
    onehot = flat_ids[:, None] == jnp.arange(experts, dtype=jnp.int32)[None, :]
    order = jnp.arange(n, dtype=jnp.int32)
    lower = (order[None, :] < order[:, None]).astype(jnp.bfloat16)
    before = jnp.dot(lower, onehot.astype(jnp.bfloat16), preferred_element_type=jnp.float32)
    slot_of = jnp.sum(jnp.where(onehot, before, 0.0), axis=1).astype(jnp.int32)
    dest = flat_ids * capacity + slot_of
    places = jnp.arange(experts * capacity, dtype=jnp.int32)
    pick = (dest[None, :] == places[:, None]).astype(jnp.bfloat16)
    flat_gate = gate_fixed.reshape(-1)
    token_of = order // topk
    cols = jnp.stack(
        [token_of, jnp.ones_like(token_of), flat_gate // 128, flat_gate % 128], axis=1
    ).astype(jnp.bfloat16)
    got = jnp.dot(pick, cols, preferred_element_type=jnp.float32)
    used = got[:, 1] > 0.5
    table = jnp.where(used, got[:, 0], float(tok_rows)).astype(jnp.int32)
    gate_table = (got[:, 2] * 128.0 + got[:, 3]) / 65536.0
    return flat_ids, slot_of, table, gate_table


def shards(
    x_quant, x_scale, out_grad, expert_ids, gate_fixed, w_gate, s_gate, w_up, s_up, w_down, s_down
):
    tok_rows, width = x_quant.shape
    topk = expert_ids.shape[1]
    experts = lax.axis_size("expert")
    capacity = tok_rows * topk * 5 // (4 * experts)
    chunks = CHUNKS if capacity % CHUNKS == 0 else 1
    per = capacity // chunks
    sub = width // LANES
    blk_width = width // x_scale.shape[1]
    flat_ids, slot_of, table, gate_table = routing(expert_ids, gate_fixed, experts, capacity)
    scaled = x_quant.reshape(tok_rows, -1, blk_width).astype(jnp.float32) * x_scale[:, :, None]
    inputs = scaled.reshape(tok_rows, sub, LANES).astype(jnp.bfloat16)
    zero_row = jnp.zeros((1, sub, LANES), jnp.bfloat16)
    input_pad = jnp.concatenate([inputs, zero_row], axis=0)
    grad_pad = jnp.concatenate([out_grad.reshape(tok_rows, sub, LANES), zero_row], axis=0)
    table = table.reshape(experts, capacity)
    gate_table = gate_table.reshape(experts, capacity)
    gate_w = dequant(w_gate[0], s_gate[0])
    up_w = dequant(w_up[0], s_up[0])
    down_w = dequant(w_down[0], s_down[0])
    rows_in = experts * per
    span = per * sub

    def payload_of(c):
        idx = table[:, c * per : (c + 1) * per]
        gates = gate_table[:, c * per : (c + 1) * per]
        send_rows = input_pad[idx]
        send_grads = (gates[:, :, None, None] * grad_pad[idx].astype(jnp.float32)).astype(jnp.bfloat16)
        return [send_rows.reshape(experts, span, LANES), send_grads.reshape(experts, span, LANES)]

    def compute(got):
        xrows = got[:, :span].reshape(rows_in, width)
        row_grad = got[:, span : 2 * span].reshape(rows_in, width)
        pre_gate, pre_up, sig, act = forward_parts(xrows, gate_w, up_w)
        hidden = (act * pre_up).astype(jnp.bfloat16)
        gate_grad, up_grad = unit_grads(row_grad, down_w, pre_gate, pre_up, sig, act)
        row_input = jnp.dot(gate_grad, gate_w.T, preferred_element_type=jnp.float32)
        row_input = row_input + jnp.dot(up_grad, up_w.T, preferred_element_type=jnp.float32)
        back_rows = row_input.astype(jnp.bfloat16).reshape(experts, span, LANES)
        return back_rows, (xrows, row_grad, hidden, gate_grad, up_grad)

    saved = []
    arrived = [None] * chunks
    backs = [None] * chunks
    returned = [None] * chunks
    for step in range(chunks + 2):
        pieces = []
        if step < chunks:
            pieces += payload_of(step)
        if step >= 2:
            pieces.append(backs[step - 2])
        got = lax.all_to_all(
            jnp.concatenate(pieces, axis=1), "expert", split_axis=0, concat_axis=0, tiled=True
        )
        if step < chunks:
            arrived[step] = got
        if step >= 2:
            returned[step - 2] = got[:, -span:]
        if 1 <= step <= chunks:
            backs[step - 1], kept = compute(arrived[step - 1])
            saved.append(kept)
    xrows, row_grad, hidden, gate_grad, up_grad = (
        jnp.concatenate(list(group), axis=0) for group in zip(*saved)
    )
    ff = gate_grad.shape[1]
    half = ff // lax.axis_size("replica")
    mine = lax.axis_index("replica")
    other = 1 - mine

    def cols(a, r):
        return lax.dynamic_slice_in_dim(a, r * half, half, axis=1)

    def weight_parts(r):
        part_gate = jnp.dot(xrows.T, cols(gate_grad, r), preferred_element_type=jnp.float32)
        part_up = jnp.dot(xrows.T, cols(up_grad, r), preferred_element_type=jnp.float32)
        part_down = jnp.dot(cols(hidden, r).T, row_grad, preferred_element_type=jnp.float32)
        return tuple(p.astype(jnp.bfloat16) for p in (part_gate, part_up, part_down))

    sent = weight_parts(other)
    kept = lax.optimization_barrier(weight_parts(mine))
    swap = [(0, 1), (1, 0)]
    came = tuple(lax.ppermute(p, "replica", swap) for p in sent)
    grad_gate, grad_up, grad_down = (
        (k.astype(jnp.float32) + c.astype(jnp.float32)).astype(jnp.bfloat16)[None]
        for k, c in zip(kept, came)
    )
    total = None
    for c in range(chunks):
        in_chunk = (slot_of // per) == c
        col = jnp.where(in_chunk, flat_ids * per + slot_of % per, -1)
        spots = jnp.arange(rows_in, dtype=jnp.int32)
        hit = (col[:, None] == spots[None, :]).astype(jnp.bfloat16)
        gather_mat = jnp.sum(hit.reshape(tok_rows, topk, rows_in), axis=1)
        back3 = returned[c].reshape(rows_in, sub, LANES)
        part = jnp.einsum("tj,jkl->tkl", gather_mat, back3, preferred_element_type=jnp.float32)
        total = part if total is None else total + part
    grad_input = total.reshape(tok_rows, width).astype(jnp.bfloat16)
    return (grad_input, grad_gate, grad_up, grad_down)


def solution(mesh):
    placed = (
        P(("expert", "replica"), None),
        P(("expert", "replica"), None),
        P(("expert", "replica"), None),
        P(("expert", "replica"), None),
        P(("expert", "replica"), None),
        P("expert", None, None),
        P("expert", None, None),
        P("expert", None, None),
        P("expert", None, None),
        P("expert", None, None),
        P("expert", None, None),
    )
    return jax.shard_map(
        shards,
        mesh=mesh,
        in_specs=placed,
        out_specs=(
            P(("expert", "replica"), None),
            P("expert", None, "replica"),
            P("expert", None, "replica"),
            P("expert", "replica", None),
        ),
        check_vma=False,
    )
```

```python
import jax
import jax.numpy as jnp
from jax import lax
from jax.sharding import PartitionSpec as P

LANES = 128
CHUNKS = 4


def dequant(weight, scale):
    rows, cols = weight.shape
    srows, scols = scale.shape
    wide = jnp.repeat(scale, cols // scols, axis=1)
    blocks = weight.reshape(srows, rows // srows, cols).astype(jnp.float32)
    return (blocks * wide[:, None, :]).reshape(rows, cols).astype(jnp.bfloat16)


def forward_parts(xrows, gate_w, up_w):
    pre_gate = jnp.dot(xrows, gate_w, preferred_element_type=jnp.float32)
    pre_up = jnp.dot(xrows, up_w, preferred_element_type=jnp.float32)
    sig = jax.nn.sigmoid(pre_gate)
    act = pre_gate * sig
    return (pre_gate, pre_up, sig, act)


def unit_grads(row_grad, down_w, pre_gate, pre_up, sig, act):
    hidden_grad = jnp.dot(row_grad, down_w.T, preferred_element_type=jnp.float32)
    up_grad = (hidden_grad * act).astype(jnp.bfloat16)
    gate_grad = (hidden_grad * pre_up * sig * (1.0 + pre_gate * (1.0 - sig))).astype(jnp.bfloat16)
    return (gate_grad, up_grad)


def routing(expert_ids, gate_fixed, experts, capacity):
    tok_rows, topk = expert_ids.shape
    n = tok_rows * topk
    flat_ids = expert_ids.reshape(-1)
    onehot = flat_ids[:, None] == jnp.arange(experts, dtype=jnp.int32)[None, :]
    order = jnp.arange(n, dtype=jnp.int32)
    lower = (order[None, :] < order[:, None]).astype(jnp.bfloat16)
    before = jnp.dot(lower, onehot.astype(jnp.bfloat16), preferred_element_type=jnp.float32)
    slot_of = jnp.sum(jnp.where(onehot, before, 0.0), axis=1).astype(jnp.int32)
    dest = flat_ids * capacity + slot_of
    places = jnp.arange(experts * capacity, dtype=jnp.int32)
    pick = (dest[None, :] == places[:, None]).astype(jnp.bfloat16)
    flat_gate = gate_fixed.reshape(-1)
    token_of = order // topk
    cols = jnp.stack(
        [token_of, jnp.ones_like(token_of), flat_gate // 128, flat_gate % 128], axis=1
    ).astype(jnp.bfloat16)
    got = jnp.dot(pick, cols, preferred_element_type=jnp.float32)
    used = got[:, 1] > 0.5
    table = jnp.where(used, got[:, 0], float(tok_rows)).astype(jnp.int32)
    gate_table = (got[:, 2] * 128.0 + got[:, 3]) / 65536.0
    return flat_ids, slot_of, table, gate_table


def shards(
    x_quant, x_scale, out_grad, expert_ids, gate_fixed, w_gate, s_gate, w_up, s_up, w_down, s_down
):
    tok_rows, width = x_quant.shape
    topk = expert_ids.shape[1]
    experts = lax.axis_size("expert")
    capacity = tok_rows * topk * 5 // (4 * experts)
    chunks = CHUNKS if capacity % CHUNKS == 0 else 1
    per = capacity // chunks
    sub = width // LANES
    blk_width = width // x_scale.shape[1]
    flat_ids, slot_of, table, gate_table = routing(expert_ids, gate_fixed, experts, capacity)
    scaled = x_quant.reshape(tok_rows, -1, blk_width).astype(jnp.float32) * x_scale[:, :, None]
    inputs = scaled.reshape(tok_rows, sub, LANES).astype(jnp.bfloat16)
    zero_row = jnp.zeros((1, sub, LANES), jnp.bfloat16)
    source = jnp.concatenate(
        [inputs, zero_row, out_grad.reshape(tok_rows, sub, LANES), zero_row], axis=0
    )
    table = table.reshape(experts, capacity)
    gate_table = gate_table.reshape(experts, capacity)
    gate_w = dequant(w_gate[0], s_gate[0])
    up_w = dequant(w_up[0], s_up[0])
    down_w = dequant(w_down[0], s_down[0])
    rows_in = experts * per
    span = per * sub

    def payload_of(c):
        idx = table[:, c * per : (c + 1) * per]
        gates = gate_table[:, c * per : (c + 1) * per]
        both = jnp.concatenate([idx, idx + (tok_rows + 1)], axis=1)
        scale = jnp.concatenate([jnp.ones_like(gates), gates], axis=1)
        rows = (scale[:, :, None, None] * source[both].astype(jnp.float32)).astype(jnp.bfloat16)
        return [rows.reshape(experts, 2 * span, LANES)]

    def compute(got):
        xrows = got[:, :span].reshape(rows_in, width)
        row_grad = got[:, span : 2 * span].reshape(rows_in, width)
        pre_gate, pre_up, sig, act = forward_parts(xrows, gate_w, up_w)
        hidden = (act * pre_up).astype(jnp.bfloat16)
        gate_grad, up_grad = unit_grads(row_grad, down_w, pre_gate, pre_up, sig, act)
        row_input = jnp.dot(gate_grad, gate_w.T, preferred_element_type=jnp.float32)
        row_input = row_input + jnp.dot(up_grad, up_w.T, preferred_element_type=jnp.float32)
        back_rows = row_input.astype(jnp.bfloat16).reshape(experts, span, LANES)
        return back_rows, (xrows, row_grad, hidden, gate_grad, up_grad)

    saved = []
    arrived = [None] * chunks
    backs = [None] * chunks
    returned = [None] * chunks
    for step in range(chunks + 2):
        pieces = []
        if step < chunks:
            pieces += payload_of(step)
        if step >= 2:
            pieces.append(backs[step - 2])
        got = lax.all_to_all(
            jnp.concatenate(pieces, axis=1), "expert", split_axis=0, concat_axis=0, tiled=True
        )
        if step < chunks:
            arrived[step] = got
        if step >= 2:
            returned[step - 2] = got[:, -span:]
        if 1 <= step <= chunks:
            backs[step - 1], kept = compute(arrived[step - 1])
            saved.append(kept)
    xrows, row_grad, hidden, gate_grad, up_grad = (
        jnp.concatenate(list(group), axis=0) for group in zip(*saved)
    )
    ff = gate_grad.shape[1]
    half = ff // lax.axis_size("replica")
    mine = lax.axis_index("replica")
    other = 1 - mine

    def cols(a, r):
        return lax.dynamic_slice_in_dim(a, r * half, half, axis=1)

    def weight_parts(r):
        part_gate = jnp.dot(xrows.T, cols(gate_grad, r), preferred_element_type=jnp.float32)
        part_up = jnp.dot(xrows.T, cols(up_grad, r), preferred_element_type=jnp.float32)
        part_down = jnp.dot(cols(hidden, r).T, row_grad, preferred_element_type=jnp.float32)
        return tuple(p.astype(jnp.bfloat16) for p in (part_gate, part_up, part_down))

    sent = weight_parts(other)
    kept = lax.optimization_barrier(weight_parts(mine))
    swap = [(0, 1), (1, 0)]
    came = tuple(lax.ppermute(p, "replica", swap) for p in sent)
    grad_gate, grad_up, grad_down = (
        (k.astype(jnp.float32) + c.astype(jnp.float32)).astype(jnp.bfloat16)[None]
        for k, c in zip(kept, came)
    )
    total = None
    for c in range(chunks):
        in_chunk = (slot_of // per) == c
        col = jnp.where(in_chunk, flat_ids * per + slot_of % per, -1)
        spots = jnp.arange(rows_in, dtype=jnp.int32)
        hit = (col[:, None] == spots[None, :]).astype(jnp.bfloat16)
        gather_mat = jnp.sum(hit.reshape(tok_rows, topk, rows_in), axis=1)
        back3 = returned[c].reshape(rows_in, sub, LANES)
        part = jnp.einsum("tj,jkl->tkl", gather_mat, back3, preferred_element_type=jnp.float32)
        total = part if total is None else total + part
    grad_input = total.reshape(tok_rows, width).astype(jnp.bfloat16)
    return (grad_input, grad_gate, grad_up, grad_down)


def solution(mesh):
    placed = (
        P(("expert", "replica"), None),
        P(("expert", "replica"), None),
        P(("expert", "replica"), None),
        P(("expert", "replica"), None),
        P(("expert", "replica"), None),
        P("expert", None, None),
        P("expert", None, None),
        P("expert", None, None),
        P("expert", None, None),
        P("expert", None, None),
        P("expert", None, None),
    )
    return jax.shard_map(
        shards,
        mesh=mesh,
        in_specs=placed,
        out_specs=(
            P(("expert", "replica"), None),
            P("expert", None, "replica"),
            P("expert", None, "replica"),
            P("expert", "replica", None),
        ),
        check_vma=False,
    )
```

```python
import jax
import jax.numpy as jnp
from jax import lax
from jax.sharding import PartitionSpec as P

LANES = 128
CHUNKS = 4


def dequant(weight, scale):
    rows, cols = weight.shape
    srows, scols = scale.shape
    wide = jnp.repeat(scale, cols // scols, axis=1)
    blocks = weight.reshape(srows, rows // srows, cols).astype(jnp.float32)
    return (blocks * wide[:, None, :]).reshape(rows, cols).astype(jnp.bfloat16)


def forward_parts(xrows, gate_w, up_w):
    pre_gate = jnp.dot(xrows, gate_w, preferred_element_type=jnp.float32)
    pre_up = jnp.dot(xrows, up_w, preferred_element_type=jnp.float32)
    sig = jax.nn.sigmoid(pre_gate)
    act = pre_gate * sig
    return (pre_gate, pre_up, sig, act)


def unit_grads(row_grad, down_w, pre_gate, pre_up, sig, act):
    hidden_grad = jnp.dot(row_grad, down_w.T, preferred_element_type=jnp.float32)
    up_grad = (hidden_grad * act).astype(jnp.bfloat16)
    gate_grad = (hidden_grad * pre_up * sig * (1.0 + pre_gate * (1.0 - sig))).astype(jnp.bfloat16)
    return (gate_grad, up_grad)


def routing(expert_ids, gate_fixed, experts, capacity):
    tok_rows, topk = expert_ids.shape
    n = tok_rows * topk
    flat_ids = expert_ids.reshape(-1)
    onehot = flat_ids[:, None] == jnp.arange(experts, dtype=jnp.int32)[None, :]
    order = jnp.arange(n, dtype=jnp.int32)
    lower = (order[None, :] < order[:, None]).astype(jnp.bfloat16)
    before = jnp.dot(lower, onehot.astype(jnp.bfloat16), preferred_element_type=jnp.float32)
    slot_of = jnp.sum(jnp.where(onehot, before, 0.0), axis=1).astype(jnp.int32)
    dest = flat_ids * capacity + slot_of
    places = jnp.arange(experts * capacity, dtype=jnp.int32)
    pick = (dest[None, :] == places[:, None]).astype(jnp.bfloat16)
    flat_gate = gate_fixed.reshape(-1)
    token_of = order // topk
    cols = jnp.stack(
        [token_of, jnp.ones_like(token_of), flat_gate // 128, flat_gate % 128], axis=1
    ).astype(jnp.bfloat16)
    got = jnp.dot(pick, cols, preferred_element_type=jnp.float32)
    used = got[:, 1] > 0.5
    table = jnp.where(used, got[:, 0], float(tok_rows)).astype(jnp.int32)
    gate_table = (got[:, 2] * 128.0 + got[:, 3]) / 65536.0
    return flat_ids, slot_of, table, gate_table


def shards(
    x_quant, x_scale, out_grad, expert_ids, gate_fixed, w_gate, s_gate, w_up, s_up, w_down, s_down
):
    tok_rows, width = x_quant.shape
    topk = expert_ids.shape[1]
    experts = lax.axis_size("expert")
    capacity = tok_rows * topk * 5 // (4 * experts)
    chunks = CHUNKS if capacity % CHUNKS == 0 else 1
    per = capacity // chunks
    sub = width // LANES
    blk_width = width // x_scale.shape[1]
    flat_ids, slot_of, table, gate_table = routing(expert_ids, gate_fixed, experts, capacity)
    scaled = x_quant.reshape(tok_rows, -1, blk_width).astype(jnp.float32) * x_scale[:, :, None]
    inputs = scaled.reshape(tok_rows, sub, LANES).astype(jnp.bfloat16)
    zero_row = jnp.zeros((1, sub, LANES), jnp.bfloat16)
    source = jnp.concatenate(
        [inputs, zero_row, out_grad.reshape(tok_rows, sub, LANES), zero_row], axis=0
    )
    table = table.reshape(experts, capacity)
    gate_table = gate_table.reshape(experts, capacity)
    gate_w = dequant(w_gate[0], s_gate[0])
    up_w = dequant(w_up[0], s_up[0])
    down_w = dequant(w_down[0], s_down[0])
    rows_in = experts * per
    span = per * sub

    def payload_of(c):
        idx = table[:, c * per : (c + 1) * per]
        gates = gate_table[:, c * per : (c + 1) * per]
        both = jnp.concatenate([idx, idx + (tok_rows + 1)], axis=1)
        scale = jnp.concatenate([jnp.ones_like(gates), gates], axis=1)
        rows = (scale[:, :, None, None] * source[both].astype(jnp.float32)).astype(jnp.bfloat16)
        return [rows.reshape(experts, 2 * span, LANES)]

    gate_w3 = gate_w.reshape(sub, LANES, -1)
    up_w3 = up_w.reshape(sub, LANES, -1)
    down_w3 = down_w.reshape(-1, sub, LANES)

    def compute(got):
        x3 = got[:, :span].reshape(rows_in, sub, LANES)
        g3 = got[:, span : 2 * span].reshape(rows_in, sub, LANES)
        pre_gate = jnp.einsum("rkl,klf->rf", x3, gate_w3, preferred_element_type=jnp.float32)
        pre_up = jnp.einsum("rkl,klf->rf", x3, up_w3, preferred_element_type=jnp.float32)
        sig = jax.nn.sigmoid(pre_gate)
        act = pre_gate * sig
        hidden = (act * pre_up).astype(jnp.bfloat16)
        hidden_grad = jnp.einsum("rkl,fkl->rf", g3, down_w3, preferred_element_type=jnp.float32)
        up_grad = (hidden_grad * act).astype(jnp.bfloat16)
        gate_grad = (hidden_grad * pre_up * sig * (1.0 + pre_gate * (1.0 - sig))).astype(jnp.bfloat16)
        row_input = jnp.einsum("rf,klf->rkl", gate_grad, gate_w3, preferred_element_type=jnp.float32)
        row_input = row_input + jnp.einsum(
            "rf,klf->rkl", up_grad, up_w3, preferred_element_type=jnp.float32
        )
        back_rows = row_input.astype(jnp.bfloat16).reshape(experts, span, LANES)
        return back_rows, (x3.reshape(rows_in, width), g3.reshape(rows_in, width), hidden, gate_grad, up_grad)

    saved = []
    arrived = [None] * chunks
    backs = [None] * chunks
    returned = [None] * chunks
    for step in range(chunks + 2):
        pieces = []
        if step < chunks:
            pieces += payload_of(step)
        if step >= 2:
            pieces.append(backs[step - 2])
        got = lax.all_to_all(
            jnp.concatenate(pieces, axis=1), "expert", split_axis=0, concat_axis=0, tiled=True
        )
        if step < chunks:
            arrived[step] = got
        if step >= 2:
            returned[step - 2] = got[:, -span:]
        if 1 <= step <= chunks:
            backs[step - 1], kept = compute(arrived[step - 1])
            saved.append(kept)
    xrows, row_grad, hidden, gate_grad, up_grad = (
        jnp.concatenate(list(group), axis=0) for group in zip(*saved)
    )
    ff = gate_grad.shape[1]
    half = ff // lax.axis_size("replica")
    mine = lax.axis_index("replica")
    other = 1 - mine

    def cols(a, r):
        return lax.dynamic_slice_in_dim(a, r * half, half, axis=1)

    def weight_parts(r):
        part_gate = jnp.dot(xrows.T, cols(gate_grad, r), preferred_element_type=jnp.float32)
        part_up = jnp.dot(xrows.T, cols(up_grad, r), preferred_element_type=jnp.float32)
        part_down = jnp.dot(cols(hidden, r).T, row_grad, preferred_element_type=jnp.float32)
        return tuple(p.astype(jnp.bfloat16) for p in (part_gate, part_up, part_down))

    sent = weight_parts(other)
    kept = lax.optimization_barrier(weight_parts(mine))
    swap = [(0, 1), (1, 0)]
    came = tuple(lax.ppermute(p, "replica", swap) for p in sent)
    grad_gate, grad_up, grad_down = (
        (k.astype(jnp.float32) + c.astype(jnp.float32)).astype(jnp.bfloat16)[None]
        for k, c in zip(kept, came)
    )
    total = None
    for c in range(chunks):
        in_chunk = (slot_of // per) == c
        col = jnp.where(in_chunk, flat_ids * per + slot_of % per, -1)
        spots = jnp.arange(rows_in, dtype=jnp.int32)
        hit = (col[:, None] == spots[None, :]).astype(jnp.bfloat16)
        gather_mat = jnp.sum(hit.reshape(tok_rows, topk, rows_in), axis=1)
        back3 = returned[c].reshape(rows_in, sub, LANES)
        part = jnp.einsum("tj,jkl->tkl", gather_mat, back3, preferred_element_type=jnp.float32)
        total = part if total is None else total + part
    grad_input = total.reshape(tok_rows, width).astype(jnp.bfloat16)
    return (grad_input, grad_gate, grad_up, grad_down)


def solution(mesh):
    placed = (
        P(("expert", "replica"), None),
        P(("expert", "replica"), None),
        P(("expert", "replica"), None),
        P(("expert", "replica"), None),
        P(("expert", "replica"), None),
        P("expert", None, None),
        P("expert", None, None),
        P("expert", None, None),
        P("expert", None, None),
        P("expert", None, None),
        P("expert", None, None),
    )
    return jax.shard_map(
        shards,
        mesh=mesh,
        in_specs=placed,
        out_specs=(
            P(("expert", "replica"), None),
            P("expert", None, "replica"),
            P("expert", None, "replica"),
            P("expert", "replica", None),
        ),
        check_vma=False,
    )
```

```python
import jax
import jax.numpy as jnp
from jax import lax
from jax.sharding import PartitionSpec as P

LANES = 128
CHUNKS = 4


def dequant(weight, scale):
    rows, cols = weight.shape
    srows, scols = scale.shape
    wide = jnp.repeat(scale, cols // scols, axis=1)
    blocks = weight.reshape(srows, rows // srows, cols).astype(jnp.float32)
    return (blocks * wide[:, None, :]).reshape(rows, cols).astype(jnp.bfloat16)


def forward_parts(xrows, gate_w, up_w):
    pre_gate = jnp.dot(xrows, gate_w, preferred_element_type=jnp.float32)
    pre_up = jnp.dot(xrows, up_w, preferred_element_type=jnp.float32)
    sig = jax.nn.sigmoid(pre_gate)
    act = pre_gate * sig
    return (pre_gate, pre_up, sig, act)


def unit_grads(row_grad, down_w, pre_gate, pre_up, sig, act):
    hidden_grad = jnp.dot(row_grad, down_w.T, preferred_element_type=jnp.float32)
    up_grad = (hidden_grad * act).astype(jnp.bfloat16)
    gate_grad = (hidden_grad * pre_up * sig * (1.0 + pre_gate * (1.0 - sig))).astype(jnp.bfloat16)
    return (gate_grad, up_grad)


def routing(expert_ids, gate_fixed, experts, capacity):
    tok_rows, topk = expert_ids.shape
    n = tok_rows * topk
    flat_ids = expert_ids.reshape(-1)
    onehot = flat_ids[:, None] == jnp.arange(experts, dtype=jnp.int32)[None, :]
    order = jnp.arange(n, dtype=jnp.int32)
    lower = (order[None, :] < order[:, None]).astype(jnp.bfloat16)
    before = jnp.dot(lower, onehot.astype(jnp.bfloat16), preferred_element_type=jnp.float32)
    slot_of = jnp.sum(jnp.where(onehot, before, 0.0), axis=1).astype(jnp.int32)
    dest = flat_ids * capacity + slot_of
    places = jnp.arange(experts * capacity, dtype=jnp.int32)
    pick = (dest[None, :] == places[:, None]).astype(jnp.bfloat16)
    flat_gate = gate_fixed.reshape(-1)
    token_of = order // topk
    cols = jnp.stack(
        [token_of, jnp.ones_like(token_of), flat_gate // 128, flat_gate % 128], axis=1
    ).astype(jnp.bfloat16)
    got = jnp.dot(pick, cols, preferred_element_type=jnp.float32)
    used = got[:, 1] > 0.5
    table = jnp.where(used, got[:, 0], float(tok_rows)).astype(jnp.int32)
    gate_table = (got[:, 2] * 128.0 + got[:, 3]) / 65536.0
    return flat_ids, slot_of, table, gate_table


def shards(
    x_quant, x_scale, out_grad, expert_ids, gate_fixed, w_gate, s_gate, w_up, s_up, w_down, s_down
):
    tok_rows, width = x_quant.shape
    topk = expert_ids.shape[1]
    experts = lax.axis_size("expert")
    capacity = tok_rows * topk * 5 // (4 * experts)
    last = max(1, capacity // 10)
    lead = [(capacity - last) // (CHUNKS - 1)] * (CHUNKS - 1)
    lead[-1] += capacity - last - sum(lead)
    sizes = lead + [last]
    bounds = [sum(sizes[:c]) for c in range(CHUNKS + 1)]
    chunks = CHUNKS
    sub = width // LANES
    blk_width = width // x_scale.shape[1]
    flat_ids, slot_of, table, gate_table = routing(expert_ids, gate_fixed, experts, capacity)
    scaled = x_quant.reshape(tok_rows, -1, blk_width).astype(jnp.float32) * x_scale[:, :, None]
    inputs = scaled.reshape(tok_rows, sub, LANES).astype(jnp.bfloat16)
    zero_row = jnp.zeros((1, sub, LANES), jnp.bfloat16)
    source = jnp.concatenate(
        [inputs, zero_row, out_grad.reshape(tok_rows, sub, LANES), zero_row], axis=0
    )
    table = table.reshape(experts, capacity)
    gate_table = gate_table.reshape(experts, capacity)
    gate_w = dequant(w_gate[0], s_gate[0])
    up_w = dequant(w_up[0], s_up[0])
    down_w = dequant(w_down[0], s_down[0])

    def payload_of(c):
        idx = table[:, bounds[c] : bounds[c + 1]]
        gates = gate_table[:, bounds[c] : bounds[c + 1]]
        span = sizes[c] * sub
        both = jnp.concatenate([idx, idx + (tok_rows + 1)], axis=1)
        scale = jnp.concatenate([jnp.ones_like(gates), gates], axis=1)
        rows = (scale[:, :, None, None] * source[both].astype(jnp.float32)).astype(jnp.bfloat16)
        return [rows.reshape(experts, 2 * span, LANES)]

    gate_w3 = gate_w.reshape(sub, LANES, -1)
    up_w3 = up_w.reshape(sub, LANES, -1)
    down_w3 = down_w.reshape(-1, sub, LANES)

    def compute(got, c):
        span = sizes[c] * sub
        rows_in = experts * sizes[c]
        x3 = got[:, :span].reshape(rows_in, sub, LANES)
        g3 = got[:, span : 2 * span].reshape(rows_in, sub, LANES)
        pre_gate = jnp.einsum("rkl,klf->rf", x3, gate_w3, preferred_element_type=jnp.float32)
        pre_up = jnp.einsum("rkl,klf->rf", x3, up_w3, preferred_element_type=jnp.float32)
        sig = jax.nn.sigmoid(pre_gate)
        act = pre_gate * sig
        hidden = (act * pre_up).astype(jnp.bfloat16)
        hidden_grad = jnp.einsum("rkl,fkl->rf", g3, down_w3, preferred_element_type=jnp.float32)
        up_grad = (hidden_grad * act).astype(jnp.bfloat16)
        gate_grad = (hidden_grad * pre_up * sig * (1.0 + pre_gate * (1.0 - sig))).astype(jnp.bfloat16)
        row_input = jnp.einsum("rf,klf->rkl", gate_grad, gate_w3, preferred_element_type=jnp.float32)
        row_input = row_input + jnp.einsum(
            "rf,klf->rkl", up_grad, up_w3, preferred_element_type=jnp.float32
        )
        back_rows = row_input.astype(jnp.bfloat16).reshape(experts, span, LANES)
        return back_rows, (x3.reshape(rows_in, width), g3.reshape(rows_in, width), hidden, gate_grad, up_grad)

    saved = []
    arrived = [None] * chunks
    backs = [None] * chunks
    returned = [None] * chunks
    for step in range(chunks + 2):
        pieces = []
        if step < chunks:
            pieces += payload_of(step)
        if step >= 2:
            pieces.append(backs[step - 2])
        got = lax.all_to_all(
            jnp.concatenate(pieces, axis=1), "expert", split_axis=0, concat_axis=0, tiled=True
        )
        if step < chunks:
            arrived[step] = got
        if step >= 2:
            returned[step - 2] = got[:, -sizes[step - 2] * sub :]
        if 1 <= step <= chunks:
            backs[step - 1], kept = compute(arrived[step - 1], step - 1)
            saved.append(kept)
    xrows, row_grad, hidden, gate_grad, up_grad = (
        jnp.concatenate(list(group), axis=0) for group in zip(*saved)
    )
    ff = gate_grad.shape[1]
    half = ff // lax.axis_size("replica")
    mine = lax.axis_index("replica")
    other = 1 - mine

    def cols(a, r):
        return lax.dynamic_slice_in_dim(a, r * half, half, axis=1)

    def weight_parts(r):
        part_gate = jnp.dot(xrows.T, cols(gate_grad, r), preferred_element_type=jnp.float32)
        part_up = jnp.dot(xrows.T, cols(up_grad, r), preferred_element_type=jnp.float32)
        part_down = jnp.dot(cols(hidden, r).T, row_grad, preferred_element_type=jnp.float32)
        return tuple(p.astype(jnp.bfloat16) for p in (part_gate, part_up, part_down))

    sent = weight_parts(other)
    kept = lax.optimization_barrier(weight_parts(mine))
    swap = [(0, 1), (1, 0)]
    came = tuple(lax.ppermute(p, "replica", swap) for p in sent)
    grad_gate, grad_up, grad_down = (
        (k.astype(jnp.float32) + c.astype(jnp.float32)).astype(jnp.bfloat16)[None]
        for k, c in zip(kept, came)
    )
    total = None
    for c in range(chunks):
        per = sizes[c]
        rows_in = experts * per
        in_chunk = (slot_of >= bounds[c]) & (slot_of < bounds[c + 1])
        col = jnp.where(in_chunk, flat_ids * per + slot_of - bounds[c], -1)
        spots = jnp.arange(rows_in, dtype=jnp.int32)
        hit = (col[:, None] == spots[None, :]).astype(jnp.bfloat16)
        gather_mat = jnp.sum(hit.reshape(tok_rows, topk, rows_in), axis=1)
        back3 = returned[c].reshape(rows_in, sub, LANES)
        part = jnp.einsum("tj,jkl->tkl", gather_mat, back3, preferred_element_type=jnp.float32)
        total = part if total is None else total + part
    grad_input = total.reshape(tok_rows, width).astype(jnp.bfloat16)
    return (grad_input, grad_gate, grad_up, grad_down)


def solution(mesh):
    placed = (
        P(("expert", "replica"), None),
        P(("expert", "replica"), None),
        P(("expert", "replica"), None),
        P(("expert", "replica"), None),
        P(("expert", "replica"), None),
        P("expert", None, None),
        P("expert", None, None),
        P("expert", None, None),
        P("expert", None, None),
        P("expert", None, None),
        P("expert", None, None),
    )
    return jax.shard_map(
        shards,
        mesh=mesh,
        in_specs=placed,
        out_specs=(
            P(("expert", "replica"), None),
            P("expert", None, "replica"),
            P("expert", None, "replica"),
            P("expert", "replica", None),
        ),
        check_vma=False,
    )
```

```python
import jax
import jax.numpy as jnp
from jax import lax
from jax.sharding import PartitionSpec as P

LANES = 128
CHUNKS = 4


def dequant(weight, scale):
    rows, cols = weight.shape
    srows, scols = scale.shape
    wide = jnp.repeat(scale, cols // scols, axis=1)
    blocks = weight.reshape(srows, rows // srows, cols).astype(jnp.float32)
    return (blocks * wide[:, None, :]).reshape(rows, cols).astype(jnp.bfloat16)


def forward_parts(xrows, gate_w, up_w):
    pre_gate = jnp.dot(xrows, gate_w, preferred_element_type=jnp.float32)
    pre_up = jnp.dot(xrows, up_w, preferred_element_type=jnp.float32)
    sig = jax.nn.sigmoid(pre_gate)
    act = pre_gate * sig
    return (pre_gate, pre_up, sig, act)


def unit_grads(row_grad, down_w, pre_gate, pre_up, sig, act):
    hidden_grad = jnp.dot(row_grad, down_w.T, preferred_element_type=jnp.float32)
    up_grad = (hidden_grad * act).astype(jnp.bfloat16)
    gate_grad = (hidden_grad * pre_up * sig * (1.0 + pre_gate * (1.0 - sig))).astype(jnp.bfloat16)
    return (gate_grad, up_grad)


def routing(expert_ids, gate_fixed, experts, capacity):
    tok_rows, topk = expert_ids.shape
    n = tok_rows * topk
    flat_ids = expert_ids.reshape(-1)
    onehot = flat_ids[:, None] == jnp.arange(experts, dtype=jnp.int32)[None, :]
    order = jnp.arange(n, dtype=jnp.int32)
    lower = (order[None, :] < order[:, None]).astype(jnp.bfloat16)
    before = jnp.dot(lower, onehot.astype(jnp.bfloat16), preferred_element_type=jnp.float32)
    slot_of = jnp.sum(jnp.where(onehot, before, 0.0), axis=1).astype(jnp.int32)
    dest = flat_ids * capacity + slot_of
    places = jnp.arange(experts * capacity, dtype=jnp.int32)
    pick = (dest[None, :] == places[:, None]).astype(jnp.bfloat16)
    flat_gate = gate_fixed.reshape(-1)
    token_of = order // topk
    cols = jnp.stack(
        [token_of, jnp.ones_like(token_of), flat_gate // 128, flat_gate % 128], axis=1
    ).astype(jnp.bfloat16)
    got = jnp.dot(pick, cols, preferred_element_type=jnp.float32)
    used = got[:, 1] > 0.5
    table = jnp.where(used, got[:, 0], float(tok_rows)).astype(jnp.int32)
    gate_table = (got[:, 2] * 128.0 + got[:, 3]) / 65536.0
    return flat_ids, slot_of, table, gate_table


def shards(
    x_quant, x_scale, out_grad, expert_ids, gate_fixed, w_gate, s_gate, w_up, s_up, w_down, s_down
):
    tok_rows, width = x_quant.shape
    topk = expert_ids.shape[1]
    experts = lax.axis_size("expert")
    capacity = tok_rows * topk * 5 // (4 * experts)
    chunks = CHUNKS if capacity % CHUNKS == 0 else 1
    per = capacity // chunks
    sub = width // LANES
    blk_width = width // x_scale.shape[1]
    flat_ids, slot_of, table, gate_table = routing(expert_ids, gate_fixed, experts, capacity)
    scaled = x_quant.reshape(tok_rows, -1, blk_width).astype(jnp.float32) * x_scale[:, :, None]
    inputs = scaled.reshape(tok_rows, sub, LANES).astype(jnp.bfloat16)
    zero_row = jnp.zeros((1, sub, LANES), jnp.bfloat16)
    source = jnp.concatenate(
        [inputs, zero_row, out_grad.reshape(tok_rows, sub, LANES), zero_row], axis=0
    )
    table = table.reshape(experts, capacity)
    gate_table = gate_table.reshape(experts, capacity)
    gate_w = dequant(w_gate[0], s_gate[0])
    up_w = dequant(w_up[0], s_up[0])
    down_w = dequant(w_down[0], s_down[0])
    rows_in = experts * per
    span = per * sub

    def payload_of(c):
        idx = table[:, c * per : (c + 1) * per]
        gates = gate_table[:, c * per : (c + 1) * per]
        both = jnp.concatenate([idx, idx + (tok_rows + 1)], axis=1)
        scale = jnp.concatenate([jnp.ones_like(gates), gates], axis=1)
        rows = (scale[:, :, None, None] * source[both].astype(jnp.float32)).astype(jnp.bfloat16)
        return [rows.reshape(experts, 2 * span, LANES)]

    both_w3 = jnp.concatenate([gate_w, up_w], axis=1).reshape(sub, LANES, -1)
    down_w3 = down_w.reshape(-1, sub, LANES)

    def compute(got):
        x3 = got[:, :span].reshape(rows_in, sub, LANES)
        g3 = got[:, span : 2 * span].reshape(rows_in, sub, LANES)
        pre = jnp.einsum("rkl,klf->rf", x3, both_w3, preferred_element_type=jnp.float32)
        ff = pre.shape[1] // 2
        pre_gate, pre_up = pre[:, :ff], pre[:, ff:]
        sig = jax.nn.sigmoid(pre_gate)
        act = pre_gate * sig
        hidden = (act * pre_up).astype(jnp.bfloat16)
        hidden_grad = jnp.einsum("rkl,fkl->rf", g3, down_w3, preferred_element_type=jnp.float32)
        up_grad = (hidden_grad * act).astype(jnp.bfloat16)
        gate_grad = (hidden_grad * pre_up * sig * (1.0 + pre_gate * (1.0 - sig))).astype(jnp.bfloat16)
        unit_grad = jnp.concatenate([gate_grad, up_grad], axis=1)
        row_input = jnp.einsum("rf,klf->rkl", unit_grad, both_w3, preferred_element_type=jnp.float32)
        back_rows = row_input.astype(jnp.bfloat16).reshape(experts, span, LANES)
        return back_rows, (x3.reshape(rows_in, width), g3.reshape(rows_in, width), hidden, gate_grad, up_grad)

    saved = []
    arrived = [None] * chunks
    backs = [None] * chunks
    returned = [None] * chunks
    for step in range(chunks + 2):
        pieces = []
        if step < chunks:
            pieces += payload_of(step)
        if step >= 2:
            pieces.append(backs[step - 2])
        got = lax.all_to_all(
            jnp.concatenate(pieces, axis=1), "expert", split_axis=0, concat_axis=0, tiled=True
        )
        if step < chunks:
            arrived[step] = got
        if step >= 2:
            returned[step - 2] = got[:, -span:]
        if 1 <= step <= chunks:
            backs[step - 1], kept = compute(arrived[step - 1])
            saved.append(kept)
    xrows, row_grad, hidden, gate_grad, up_grad = (
        jnp.concatenate(list(group), axis=0) for group in zip(*saved)
    )
    ff = gate_grad.shape[1]
    half = ff // lax.axis_size("replica")
    mine = lax.axis_index("replica")
    other = 1 - mine

    def cols(a, r):
        return lax.dynamic_slice_in_dim(a, r * half, half, axis=1)

    def weight_parts(r):
        part_gate = jnp.dot(xrows.T, cols(gate_grad, r), preferred_element_type=jnp.float32)
        part_up = jnp.dot(xrows.T, cols(up_grad, r), preferred_element_type=jnp.float32)
        part_down = jnp.dot(cols(hidden, r).T, row_grad, preferred_element_type=jnp.float32)
        return tuple(p.astype(jnp.bfloat16) for p in (part_gate, part_up, part_down))

    sent = weight_parts(other)
    kept = lax.optimization_barrier(weight_parts(mine))
    swap = [(0, 1), (1, 0)]
    came = tuple(lax.ppermute(p, "replica", swap) for p in sent)
    grad_gate, grad_up, grad_down = (
        (k.astype(jnp.float32) + c.astype(jnp.float32)).astype(jnp.bfloat16)[None]
        for k, c in zip(kept, came)
    )
    total = None
    for c in range(chunks):
        in_chunk = (slot_of // per) == c
        col = jnp.where(in_chunk, flat_ids * per + slot_of % per, -1)
        spots = jnp.arange(rows_in, dtype=jnp.int32)
        hit = (col[:, None] == spots[None, :]).astype(jnp.bfloat16)
        gather_mat = jnp.sum(hit.reshape(tok_rows, topk, rows_in), axis=1)
        back3 = returned[c].reshape(rows_in, sub, LANES)
        part = jnp.einsum("tj,jkl->tkl", gather_mat, back3, preferred_element_type=jnp.float32)
        total = part if total is None else total + part
    grad_input = total.reshape(tok_rows, width).astype(jnp.bfloat16)
    return (grad_input, grad_gate, grad_up, grad_down)


def solution(mesh):
    placed = (
        P(("expert", "replica"), None),
        P(("expert", "replica"), None),
        P(("expert", "replica"), None),
        P(("expert", "replica"), None),
        P(("expert", "replica"), None),
        P("expert", None, None),
        P("expert", None, None),
        P("expert", None, None),
        P("expert", None, None),
        P("expert", None, None),
        P("expert", None, None),
    )
    return jax.shard_map(
        shards,
        mesh=mesh,
        in_specs=placed,
        out_specs=(
            P(("expert", "replica"), None),
            P("expert", None, "replica"),
            P("expert", None, "replica"),
            P("expert", "replica", None),
        ),
        check_vma=False,
    )
```

```python
import jax
import jax.numpy as jnp
from jax import lax
from jax.sharding import PartitionSpec as P

LANES = 128
CHUNKS = 4


def dequant(weight, scale):
    rows, cols = weight.shape
    srows, scols = scale.shape
    wide = jnp.repeat(scale, cols // scols, axis=1)
    blocks = weight.reshape(srows, rows // srows, cols).astype(jnp.float32)
    return (blocks * wide[:, None, :]).reshape(rows, cols).astype(jnp.bfloat16)


def forward_parts(xrows, gate_w, up_w):
    pre_gate = jnp.dot(xrows, gate_w, preferred_element_type=jnp.float32)
    pre_up = jnp.dot(xrows, up_w, preferred_element_type=jnp.float32)
    sig = jax.nn.sigmoid(pre_gate)
    act = pre_gate * sig
    return (pre_gate, pre_up, sig, act)


def unit_grads(row_grad, down_w, pre_gate, pre_up, sig, act):
    hidden_grad = jnp.dot(row_grad, down_w.T, preferred_element_type=jnp.float32)
    up_grad = (hidden_grad * act).astype(jnp.bfloat16)
    gate_grad = (hidden_grad * pre_up * sig * (1.0 + pre_gate * (1.0 - sig))).astype(jnp.bfloat16)
    return (gate_grad, up_grad)


def routing(expert_ids, gate_fixed, experts, capacity):
    tok_rows, topk = expert_ids.shape
    n = tok_rows * topk
    flat_ids = expert_ids.reshape(-1)
    onehot = flat_ids[:, None] == jnp.arange(experts, dtype=jnp.int32)[None, :]
    order = jnp.arange(n, dtype=jnp.int32)
    lower = (order[None, :] < order[:, None]).astype(jnp.bfloat16)
    before = jnp.dot(lower, onehot.astype(jnp.bfloat16), preferred_element_type=jnp.float32)
    slot_of = jnp.sum(jnp.where(onehot, before, 0.0), axis=1).astype(jnp.int32)
    dest = flat_ids * capacity + slot_of
    places = jnp.arange(experts * capacity, dtype=jnp.int32)
    pick = (dest[None, :] == places[:, None]).astype(jnp.bfloat16)
    flat_gate = gate_fixed.reshape(-1)
    token_of = order // topk
    cols = jnp.stack(
        [token_of, jnp.ones_like(token_of), flat_gate // 128, flat_gate % 128], axis=1
    ).astype(jnp.bfloat16)
    got = jnp.dot(pick, cols, preferred_element_type=jnp.float32)
    used = got[:, 1] > 0.5
    table = jnp.where(used, got[:, 0], float(tok_rows)).astype(jnp.int32)
    gate_table = (got[:, 2] * 128.0 + got[:, 3]) / 65536.0
    return flat_ids, slot_of, table, gate_table


def shards(
    x_quant, x_scale, out_grad, expert_ids, gate_fixed, w_gate, s_gate, w_up, s_up, w_down, s_down
):
    tok_rows, width = x_quant.shape
    topk = expert_ids.shape[1]
    experts = lax.axis_size("expert")
    capacity = tok_rows * topk * 5 // (4 * experts)
    chunks = CHUNKS if capacity % CHUNKS == 0 else 1
    per = capacity // chunks
    sub = width // LANES
    blk_width = width // x_scale.shape[1]
    flat_ids, slot_of, table, gate_table = routing(expert_ids, gate_fixed, experts, capacity)
    scaled = x_quant.reshape(tok_rows, -1, blk_width).astype(jnp.float32) * x_scale[:, :, None]
    inputs = scaled.reshape(tok_rows, sub, LANES).astype(jnp.bfloat16)
    zero_row = jnp.zeros((1, sub, LANES), jnp.bfloat16)
    source = jnp.concatenate(
        [inputs, zero_row, out_grad.reshape(tok_rows, sub, LANES), zero_row], axis=0
    )
    table = table.reshape(experts, capacity)
    gate_table = gate_table.reshape(experts, capacity)
    gate_w = dequant(w_gate[0], s_gate[0])
    up_w = dequant(w_up[0], s_up[0])
    down_w = dequant(w_down[0], s_down[0])
    rows_in = experts * per
    span = per * sub

    def payload_of(c):
        idx = table[:, c * per : (c + 1) * per]
        gates = gate_table[:, c * per : (c + 1) * per]
        both = jnp.concatenate([idx, idx + (tok_rows + 1)], axis=1)
        scale = jnp.concatenate([jnp.ones_like(gates), gates], axis=1)
        rows = (scale[:, :, None, None] * source[both].astype(jnp.float32)).astype(jnp.bfloat16)
        return [rows.reshape(experts, 2 * span, LANES)]

    both_w3 = jnp.concatenate([gate_w, up_w], axis=1).reshape(sub, LANES, -1)
    down_w3 = down_w.reshape(-1, sub, LANES)

    def compute(got):
        x3 = got[:, :span].reshape(rows_in, sub, LANES)
        g3 = got[:, span : 2 * span].reshape(rows_in, sub, LANES)
        pre = jnp.einsum("rkl,klf->rf", x3, both_w3, preferred_element_type=jnp.float32)
        ff = pre.shape[1] // 2
        pre_gate, pre_up = pre[:, :ff], pre[:, ff:]
        sig = jax.nn.sigmoid(pre_gate)
        act = pre_gate * sig
        hidden = (act * pre_up).astype(jnp.bfloat16)
        hidden_grad = jnp.einsum("rkl,fkl->rf", g3, down_w3, preferred_element_type=jnp.float32)
        up_grad = (hidden_grad * act).astype(jnp.bfloat16)
        gate_grad = (hidden_grad * pre_up * sig * (1.0 + pre_gate * (1.0 - sig))).astype(jnp.bfloat16)
        unit_grad = jnp.concatenate([gate_grad, up_grad], axis=1)
        row_input = jnp.einsum("rf,klf->rkl", unit_grad, both_w3, preferred_element_type=jnp.float32)
        back_rows = row_input.astype(jnp.bfloat16).reshape(experts, span, LANES)
        return back_rows, (x3.reshape(rows_in, width), g3.reshape(rows_in, width), hidden, gate_grad, up_grad)

    def weight_parts_of(group, r, half):
        xrows, row_grad, hidden, gate_grad, up_grad = group
        pick = lambda a: lax.dynamic_slice_in_dim(a, r * half, half, axis=1)
        part_gate = jnp.dot(xrows.T, pick(gate_grad), preferred_element_type=jnp.float32)
        part_up = jnp.dot(xrows.T, pick(up_grad), preferred_element_type=jnp.float32)
        part_down = jnp.dot(pick(hidden).T, row_grad, preferred_element_type=jnp.float32)
        return (part_gate, part_up, part_down)

    early_chunks = chunks // 2
    saved = []
    arrived = [None] * chunks
    backs = [None] * chunks
    returned = [None] * chunks
    for step in range(chunks + 2):
        pieces = []
        if step < chunks:
            pieces += payload_of(step)
        if step >= 2:
            pieces.append(backs[step - 2])
        got = lax.all_to_all(
            jnp.concatenate(pieces, axis=1), "expert", split_axis=0, concat_axis=0, tiled=True
        )
        if step < chunks:
            arrived[step] = got
        if step >= 2:
            returned[step - 2] = got[:, -span:]
        if 1 <= step <= chunks:
            backs[step - 1], kept = compute(arrived[step - 1])
            saved.append(kept)
        if step == early_chunks:
            early = tuple(jnp.concatenate(list(g), axis=0) for g in zip(*saved))
            half = early[3].shape[1] // lax.axis_size("replica")
            mine = lax.axis_index("replica")
            early_kept, early_sent = (
                weight_parts_of(early, mine, half), weight_parts_of(early, 1 - mine, half)
            )
            backs[step - 1], early_kept, early_sent = lax.optimization_barrier(
                (backs[step - 1], early_kept, early_sent)
            )
    ff = saved[0][3].shape[1]
    half = ff // lax.axis_size("replica")
    mine = lax.axis_index("replica")
    other = 1 - mine

    def cols(a, r):
        return lax.dynamic_slice_in_dim(a, r * half, half, axis=1)

    def weight_parts(group, r):
        xrows, row_grad, hidden, gate_grad, up_grad = group
        part_gate = jnp.dot(xrows.T, cols(gate_grad, r), preferred_element_type=jnp.float32)
        part_up = jnp.dot(xrows.T, cols(up_grad, r), preferred_element_type=jnp.float32)
        part_down = jnp.dot(cols(hidden, r).T, row_grad, preferred_element_type=jnp.float32)
        return (part_gate, part_up, part_down)

    late = tuple(jnp.concatenate(list(g), axis=0) for g in zip(*saved[early_chunks:]))
    sent = tuple(
        (a + b).astype(jnp.bfloat16) for a, b in zip(early_sent, weight_parts(late, other))
    )
    kept = lax.optimization_barrier(
        tuple((a + b).astype(jnp.bfloat16) for a, b in zip(early_kept, weight_parts(late, mine)))
    )
    swap = [(0, 1), (1, 0)]
    came = tuple(lax.ppermute(p, "replica", swap) for p in sent)
    grad_gate, grad_up, grad_down = (
        (k.astype(jnp.float32) + c.astype(jnp.float32)).astype(jnp.bfloat16)[None]
        for k, c in zip(kept, came)
    )
    total = None
    for c in range(chunks):
        in_chunk = (slot_of // per) == c
        col = jnp.where(in_chunk, flat_ids * per + slot_of % per, -1)
        spots = jnp.arange(rows_in, dtype=jnp.int32)
        hit = (col[:, None] == spots[None, :]).astype(jnp.bfloat16)
        gather_mat = jnp.sum(hit.reshape(tok_rows, topk, rows_in), axis=1)
        back3 = returned[c].reshape(rows_in, sub, LANES)
        part = jnp.einsum("tj,jkl->tkl", gather_mat, back3, preferred_element_type=jnp.float32)
        total = part if total is None else total + part
    grad_input = total.reshape(tok_rows, width).astype(jnp.bfloat16)
    return (grad_input, grad_gate, grad_up, grad_down)


def solution(mesh):
    placed = (
        P(("expert", "replica"), None),
        P(("expert", "replica"), None),
        P(("expert", "replica"), None),
        P(("expert", "replica"), None),
        P(("expert", "replica"), None),
        P("expert", None, None),
        P("expert", None, None),
        P("expert", None, None),
        P("expert", None, None),
        P("expert", None, None),
        P("expert", None, None),
    )
    return jax.shard_map(
        shards,
        mesh=mesh,
        in_specs=placed,
        out_specs=(
            P(("expert", "replica"), None),
            P("expert", None, "replica"),
            P("expert", None, "replica"),
            P("expert", "replica", None),
        ),
        check_vma=False,
    )
```

```python
import jax
import jax.numpy as jnp
from jax import lax
from jax.sharding import PartitionSpec as P

LANES = 128
CHUNKS = 4


def dequant(weight, scale):
    rows, cols = weight.shape
    srows, scols = scale.shape
    wide = jnp.repeat(scale, cols // scols, axis=1)
    blocks = weight.reshape(srows, rows // srows, cols).astype(jnp.float32)
    return (blocks * wide[:, None, :]).reshape(rows, cols).astype(jnp.bfloat16)


def forward_parts(xrows, gate_w, up_w):
    pre_gate = jnp.dot(xrows, gate_w, preferred_element_type=jnp.float32)
    pre_up = jnp.dot(xrows, up_w, preferred_element_type=jnp.float32)
    sig = jax.nn.sigmoid(pre_gate)
    act = pre_gate * sig
    return (pre_gate, pre_up, sig, act)


def unit_grads(row_grad, down_w, pre_gate, pre_up, sig, act):
    hidden_grad = jnp.dot(row_grad, down_w.T, preferred_element_type=jnp.float32)
    up_grad = (hidden_grad * act).astype(jnp.bfloat16)
    gate_grad = (hidden_grad * pre_up * sig * (1.0 + pre_gate * (1.0 - sig))).astype(jnp.bfloat16)
    return (gate_grad, up_grad)


def routing(expert_ids, gate_fixed, experts, capacity):
    tok_rows, topk = expert_ids.shape
    n = tok_rows * topk
    flat_ids = expert_ids.reshape(-1)
    onehot = flat_ids[:, None] == jnp.arange(experts, dtype=jnp.int32)[None, :]
    order = jnp.arange(n, dtype=jnp.int32)
    lower = (order[None, :] < order[:, None]).astype(jnp.bfloat16)
    before = jnp.dot(lower, onehot.astype(jnp.bfloat16), preferred_element_type=jnp.float32)
    slot_of = jnp.sum(jnp.where(onehot, before, 0.0), axis=1).astype(jnp.int32)
    dest = flat_ids * capacity + slot_of
    places = jnp.arange(experts * capacity, dtype=jnp.int32)
    pick = (dest[None, :] == places[:, None]).astype(jnp.bfloat16)
    flat_gate = gate_fixed.reshape(-1)
    token_of = order // topk
    cols = jnp.stack(
        [token_of, jnp.ones_like(token_of), flat_gate // 128, flat_gate % 128], axis=1
    ).astype(jnp.bfloat16)
    got = jnp.dot(pick, cols, preferred_element_type=jnp.float32)
    used = got[:, 1] > 0.5
    table = jnp.where(used, got[:, 0], float(tok_rows)).astype(jnp.int32)
    gate_table = (got[:, 2] * 128.0 + got[:, 3]) / 65536.0
    return flat_ids, slot_of, table, gate_table


def shards(
    x_quant, x_scale, out_grad, expert_ids, gate_fixed, w_gate, s_gate, w_up, s_up, w_down, s_down
):
    tok_rows, width = x_quant.shape
    topk = expert_ids.shape[1]
    experts = lax.axis_size("expert")
    capacity = tok_rows * topk * 5 // (4 * experts)
    chunks = CHUNKS if capacity % CHUNKS == 0 else 1
    per = capacity // chunks
    sub = width // LANES
    blk_width = width // x_scale.shape[1]
    flat_ids, slot_of, table, gate_table = routing(expert_ids, gate_fixed, experts, capacity)
    scaled = x_quant.reshape(tok_rows, -1, blk_width).astype(jnp.float32) * x_scale[:, :, None]
    inputs = scaled.reshape(tok_rows, sub, LANES).astype(jnp.bfloat16)
    zero_row = jnp.zeros((1, sub, LANES), jnp.bfloat16)
    source = jnp.concatenate(
        [inputs, zero_row, out_grad.reshape(tok_rows, sub, LANES), zero_row], axis=0
    )
    table = table.reshape(experts, capacity)
    gate_table = gate_table.reshape(experts, capacity)
    gate_w = dequant(w_gate[0], s_gate[0])
    up_w = dequant(w_up[0], s_up[0])
    down_w = dequant(w_down[0], s_down[0])
    rows_in = experts * per
    span = per * sub

    def payload_of(c):
        idx = table[:, c * per : (c + 1) * per]
        gates = gate_table[:, c * per : (c + 1) * per]
        both = jnp.concatenate([idx, idx + (tok_rows + 1)], axis=1)
        scale = jnp.concatenate([jnp.ones_like(gates), gates], axis=1)
        rows = (scale[:, :, None, None] * source[both].astype(jnp.float32)).astype(jnp.bfloat16)
        return [rows.reshape(experts, 2 * span, LANES)]

    both_w3 = jnp.concatenate([gate_w, up_w], axis=1).reshape(sub, LANES, -1)
    down_w3 = down_w.reshape(-1, sub, LANES)

    def compute(got):
        x3 = got[:, :span].reshape(rows_in, sub, LANES)
        g3 = got[:, span : 2 * span].reshape(rows_in, sub, LANES)
        pre = jnp.einsum("rkl,klf->rf", x3, both_w3, preferred_element_type=jnp.float32)
        ff = pre.shape[1] // 2
        pre_gate, pre_up = pre[:, :ff], pre[:, ff:]
        sig = jax.nn.sigmoid(pre_gate)
        act = pre_gate * sig
        hidden = (act * pre_up).astype(jnp.bfloat16)
        hidden_grad = jnp.einsum("rkl,fkl->rf", g3, down_w3, preferred_element_type=jnp.float32)
        up_grad = (hidden_grad * act).astype(jnp.bfloat16)
        gate_grad = (hidden_grad * pre_up * sig * (1.0 + pre_gate * (1.0 - sig))).astype(jnp.bfloat16)
        unit_grad = jnp.concatenate([gate_grad, up_grad], axis=1)
        row_input = jnp.einsum("rf,klf->rkl", unit_grad, both_w3, preferred_element_type=jnp.float32)
        back_rows = row_input.astype(jnp.bfloat16).reshape(experts, span, LANES)
        return back_rows, (x3.reshape(rows_in, width), g3.reshape(rows_in, width), hidden, gate_grad, up_grad)

    def weight_parts_of(group, r, half):
        xrows, row_grad, hidden, gate_grad, up_grad = group
        pick = lambda a: lax.dynamic_slice_in_dim(a, r * half, half, axis=1)
        part_gate = jnp.dot(xrows.T, pick(gate_grad), preferred_element_type=jnp.float32)
        part_up = jnp.dot(xrows.T, pick(up_grad), preferred_element_type=jnp.float32)
        part_down = jnp.dot(pick(hidden).T, row_grad, preferred_element_type=jnp.float32)
        return (part_gate, part_up, part_down)

    early_chunks = chunks - 1
    saved = []
    arrived = [None] * chunks
    backs = [None] * chunks
    returned = [None] * chunks
    for step in range(chunks + 2):
        pieces = []
        if step < chunks:
            pieces += payload_of(step)
        if step >= 2:
            pieces.append(backs[step - 2])
        got = lax.all_to_all(
            jnp.concatenate(pieces, axis=1), "expert", split_axis=0, concat_axis=0, tiled=True
        )
        if step < chunks:
            arrived[step] = got
        if step >= 2:
            returned[step - 2] = got[:, -span:]
        if 1 <= step <= chunks:
            backs[step - 1], kept = compute(arrived[step - 1])
            saved.append(kept)
        if step == early_chunks:
            early = tuple(jnp.concatenate(list(g), axis=0) for g in zip(*saved))
            half = early[3].shape[1] // lax.axis_size("replica")
            mine = lax.axis_index("replica")
            early_kept, early_sent = (
                weight_parts_of(early, mine, half), weight_parts_of(early, 1 - mine, half)
            )
            backs[step - 1], early_kept, early_sent = lax.optimization_barrier(
                (backs[step - 1], early_kept, early_sent)
            )
    ff = saved[0][3].shape[1]
    half = ff // lax.axis_size("replica")
    mine = lax.axis_index("replica")
    other = 1 - mine

    def cols(a, r):
        return lax.dynamic_slice_in_dim(a, r * half, half, axis=1)

    def weight_parts(group, r):
        xrows, row_grad, hidden, gate_grad, up_grad = group
        part_gate = jnp.dot(xrows.T, cols(gate_grad, r), preferred_element_type=jnp.float32)
        part_up = jnp.dot(xrows.T, cols(up_grad, r), preferred_element_type=jnp.float32)
        part_down = jnp.dot(cols(hidden, r).T, row_grad, preferred_element_type=jnp.float32)
        return (part_gate, part_up, part_down)

    late = tuple(jnp.concatenate(list(g), axis=0) for g in zip(*saved[early_chunks:]))
    sent = tuple(
        (a + b).astype(jnp.bfloat16) for a, b in zip(early_sent, weight_parts(late, other))
    )
    kept = lax.optimization_barrier(
        tuple((a + b).astype(jnp.bfloat16) for a, b in zip(early_kept, weight_parts(late, mine)))
    )
    swap = [(0, 1), (1, 0)]
    came = tuple(lax.ppermute(p, "replica", swap) for p in sent)
    grad_gate, grad_up, grad_down = (
        (k.astype(jnp.float32) + c.astype(jnp.float32)).astype(jnp.bfloat16)[None]
        for k, c in zip(kept, came)
    )
    total = None
    for c in range(chunks):
        in_chunk = (slot_of // per) == c
        col = jnp.where(in_chunk, flat_ids * per + slot_of % per, -1)
        spots = jnp.arange(rows_in, dtype=jnp.int32)
        hit = (col[:, None] == spots[None, :]).astype(jnp.bfloat16)
        gather_mat = jnp.sum(hit.reshape(tok_rows, topk, rows_in), axis=1)
        back3 = returned[c].reshape(rows_in, sub, LANES)
        part = jnp.einsum("tj,jkl->tkl", gather_mat, back3, preferred_element_type=jnp.float32)
        total = part if total is None else total + part
    grad_input = total.reshape(tok_rows, width).astype(jnp.bfloat16)
    return (grad_input, grad_gate, grad_up, grad_down)


def solution(mesh):
    placed = (
        P(("expert", "replica"), None),
        P(("expert", "replica"), None),
        P(("expert", "replica"), None),
        P(("expert", "replica"), None),
        P(("expert", "replica"), None),
        P("expert", None, None),
        P("expert", None, None),
        P("expert", None, None),
        P("expert", None, None),
        P("expert", None, None),
        P("expert", None, None),
    )
    return jax.shard_map(
        shards,
        mesh=mesh,
        in_specs=placed,
        out_specs=(
            P(("expert", "replica"), None),
            P("expert", None, "replica"),
            P("expert", None, "replica"),
            P("expert", "replica", None),
        ),
        check_vma=False,
    )
```

```python
import jax
import jax.numpy as jnp
from jax import lax
from jax.sharding import PartitionSpec as P

LANES = 128
CHUNKS = 4


def dequant(weight, scale):
    rows, cols = weight.shape
    srows, scols = scale.shape
    wide = jnp.repeat(scale, cols // scols, axis=1)
    blocks = weight.reshape(srows, rows // srows, cols).astype(jnp.float32)
    return (blocks * wide[:, None, :]).reshape(rows, cols).astype(jnp.bfloat16)


def forward_parts(xrows, gate_w, up_w):
    pre_gate = jnp.dot(xrows, gate_w, preferred_element_type=jnp.float32)
    pre_up = jnp.dot(xrows, up_w, preferred_element_type=jnp.float32)
    sig = jax.nn.sigmoid(pre_gate)
    act = pre_gate * sig
    return (pre_gate, pre_up, sig, act)


def unit_grads(row_grad, down_w, pre_gate, pre_up, sig, act):
    hidden_grad = jnp.dot(row_grad, down_w.T, preferred_element_type=jnp.float32)
    up_grad = (hidden_grad * act).astype(jnp.bfloat16)
    gate_grad = (hidden_grad * pre_up * sig * (1.0 + pre_gate * (1.0 - sig))).astype(jnp.bfloat16)
    return (gate_grad, up_grad)


def routing(expert_ids, gate_fixed, experts, capacity):
    tok_rows, topk = expert_ids.shape
    n = tok_rows * topk
    flat_ids = expert_ids.reshape(-1)
    onehot = flat_ids[:, None] == jnp.arange(experts, dtype=jnp.int32)[None, :]
    order = jnp.arange(n, dtype=jnp.int32)
    lower = (order[None, :] < order[:, None]).astype(jnp.bfloat16)
    before = jnp.dot(lower, onehot.astype(jnp.bfloat16), preferred_element_type=jnp.float32)
    slot_of = jnp.sum(jnp.where(onehot, before, 0.0), axis=1).astype(jnp.int32)
    dest = flat_ids * capacity + slot_of
    places = jnp.arange(experts * capacity, dtype=jnp.int32)
    pick = (dest[None, :] == places[:, None]).astype(jnp.bfloat16)
    flat_gate = gate_fixed.reshape(-1)
    token_of = order // topk
    cols = jnp.stack(
        [token_of, jnp.ones_like(token_of), flat_gate // 128, flat_gate % 128], axis=1
    ).astype(jnp.bfloat16)
    got = jnp.dot(pick, cols, preferred_element_type=jnp.float32)
    used = got[:, 1] > 0.5
    table = jnp.where(used, got[:, 0], float(tok_rows)).astype(jnp.int32)
    gate_table = (got[:, 2] * 128.0 + got[:, 3]) / 65536.0
    return flat_ids, slot_of, table, gate_table


def shards(
    x_quant, x_scale, out_grad, expert_ids, gate_fixed, w_gate, s_gate, w_up, s_up, w_down, s_down
):
    tok_rows, width = x_quant.shape
    topk = expert_ids.shape[1]
    experts = lax.axis_size("expert")
    capacity = tok_rows * topk * 5 // (4 * experts)
    chunks = CHUNKS if capacity % CHUNKS == 0 else 1
    per = capacity // chunks
    sub = width // LANES
    blk_width = width // x_scale.shape[1]
    flat_ids, slot_of, table, gate_table = routing(expert_ids, gate_fixed, experts, capacity)
    scaled = x_quant.reshape(tok_rows, -1, blk_width).astype(jnp.float32) * x_scale[:, :, None]
    inputs = scaled.reshape(tok_rows, sub, LANES).astype(jnp.bfloat16)
    zero_row = jnp.zeros((1, sub, LANES), jnp.bfloat16)
    source = jnp.concatenate(
        [inputs, zero_row, out_grad.reshape(tok_rows, sub, LANES), zero_row], axis=0
    )
    table = table.reshape(experts, capacity)
    gate_table = gate_table.reshape(experts, capacity)
    gate_w = dequant(w_gate[0], s_gate[0])
    up_w = dequant(w_up[0], s_up[0])
    down_w = dequant(w_down[0], s_down[0])
    rows_in = experts * per
    span = per * sub

    def payload_of(c):
        idx = table[:, c * per : (c + 1) * per]
        gates = gate_table[:, c * per : (c + 1) * per]
        both = jnp.concatenate([idx, idx + (tok_rows + 1)], axis=1)
        scale = jnp.concatenate([jnp.ones_like(gates), gates], axis=1)
        rows = (scale[:, :, None, None] * source[both].astype(jnp.float32)).astype(jnp.bfloat16)
        return [rows.reshape(experts, 2 * span, LANES)]

    both_w3 = jnp.concatenate([gate_w, up_w], axis=1).reshape(sub, LANES, -1)
    down_w3 = down_w.reshape(-1, sub, LANES)

    def compute(got):
        x3 = got[:, :span].reshape(rows_in, sub, LANES)
        g3 = got[:, span : 2 * span].reshape(rows_in, sub, LANES)
        pre = jnp.einsum("rkl,klf->rf", x3, both_w3, preferred_element_type=jnp.float32)
        ff = pre.shape[1] // 2
        pre_gate, pre_up = pre[:, :ff], pre[:, ff:]
        sig = jax.nn.sigmoid(pre_gate)
        act = pre_gate * sig
        hidden = (act * pre_up).astype(jnp.bfloat16)
        hidden_grad = jnp.einsum("rkl,fkl->rf", g3, down_w3, preferred_element_type=jnp.float32)
        up_grad = (hidden_grad * act).astype(jnp.bfloat16)
        gate_grad = (hidden_grad * pre_up * sig * (1.0 + pre_gate * (1.0 - sig))).astype(jnp.bfloat16)
        unit_grad = jnp.concatenate([gate_grad, up_grad], axis=1)
        row_input = jnp.einsum("rf,klf->rkl", unit_grad, both_w3, preferred_element_type=jnp.float32)
        back_rows = row_input.astype(jnp.bfloat16).reshape(experts, span, LANES)
        return back_rows, (x3.reshape(rows_in, width), g3.reshape(rows_in, width), hidden, gate_grad, up_grad)

    def weight_parts_of(group, r, half):
        xrows, row_grad, hidden, gate_grad, up_grad = group
        pick = lambda a: lax.dynamic_slice_in_dim(a, r * half, half, axis=1)
        part_gate = jnp.dot(xrows.T, pick(gate_grad), preferred_element_type=jnp.float32)
        part_up = jnp.dot(xrows.T, pick(up_grad), preferred_element_type=jnp.float32)
        part_down = jnp.dot(pick(hidden).T, row_grad, preferred_element_type=jnp.float32)
        return (part_gate, part_up, part_down)

    early_chunks = chunks - 1
    saved = []
    arrived = [None] * chunks
    backs = [None] * chunks
    returned = [None] * chunks
    for step in range(chunks + 2):
        pieces = []
        if step < chunks:
            pieces += payload_of(step)
        if step >= 2:
            pieces.append(backs[step - 2])
        got = lax.all_to_all(
            jnp.concatenate(pieces, axis=1), "expert", split_axis=0, concat_axis=0, tiled=True
        )
        if step < chunks:
            arrived[step] = got
        if step >= 2:
            returned[step - 2] = got[:, -span:]
        if 1 <= step <= chunks:
            backs[step - 1], kept = compute(arrived[step - 1])
            saved.append(kept)
        if step in (early_chunks - 1, early_chunks):
            first = 0 if step == early_chunks - 1 else early_chunks - 1
            early = tuple(jnp.concatenate(list(g), axis=0) for g in zip(*saved[first:]))
            half = early[3].shape[1] // lax.axis_size("replica")
            mine = lax.axis_index("replica")
            new_kept = weight_parts_of(early, mine, half)
            new_sent = weight_parts_of(early, 1 - mine, half)
            if first > 0:
                new_kept = tuple(a + b for a, b in zip(early_kept, new_kept))
                new_sent = tuple(a + b for a, b in zip(early_sent, new_sent))
            backs[step - 1], early_kept, early_sent = lax.optimization_barrier(
                (backs[step - 1], new_kept, new_sent)
            )
    ff = saved[0][3].shape[1]
    half = ff // lax.axis_size("replica")
    mine = lax.axis_index("replica")
    other = 1 - mine

    def cols(a, r):
        return lax.dynamic_slice_in_dim(a, r * half, half, axis=1)

    def weight_parts(group, r):
        xrows, row_grad, hidden, gate_grad, up_grad = group
        part_gate = jnp.dot(xrows.T, cols(gate_grad, r), preferred_element_type=jnp.float32)
        part_up = jnp.dot(xrows.T, cols(up_grad, r), preferred_element_type=jnp.float32)
        part_down = jnp.dot(cols(hidden, r).T, row_grad, preferred_element_type=jnp.float32)
        return (part_gate, part_up, part_down)

    late = tuple(jnp.concatenate(list(g), axis=0) for g in zip(*saved[early_chunks:]))
    sent = tuple(
        (a + b).astype(jnp.bfloat16) for a, b in zip(early_sent, weight_parts(late, other))
    )
    kept = lax.optimization_barrier(
        tuple((a + b).astype(jnp.bfloat16) for a, b in zip(early_kept, weight_parts(late, mine)))
    )
    swap = [(0, 1), (1, 0)]
    came = tuple(lax.ppermute(p, "replica", swap) for p in sent)
    grad_gate, grad_up, grad_down = (
        (k.astype(jnp.float32) + c.astype(jnp.float32)).astype(jnp.bfloat16)[None]
        for k, c in zip(kept, came)
    )
    total = None
    for c in range(chunks):
        in_chunk = (slot_of // per) == c
        col = jnp.where(in_chunk, flat_ids * per + slot_of % per, -1)
        spots = jnp.arange(rows_in, dtype=jnp.int32)
        hit = (col[:, None] == spots[None, :]).astype(jnp.bfloat16)
        gather_mat = jnp.sum(hit.reshape(tok_rows, topk, rows_in), axis=1)
        back3 = returned[c].reshape(rows_in, sub, LANES)
        part = jnp.einsum("tj,jkl->tkl", gather_mat, back3, preferred_element_type=jnp.float32)
        total = part if total is None else total + part
    grad_input = total.reshape(tok_rows, width).astype(jnp.bfloat16)
    return (grad_input, grad_gate, grad_up, grad_down)


def solution(mesh):
    placed = (
        P(("expert", "replica"), None),
        P(("expert", "replica"), None),
        P(("expert", "replica"), None),
        P(("expert", "replica"), None),
        P(("expert", "replica"), None),
        P("expert", None, None),
        P("expert", None, None),
        P("expert", None, None),
        P("expert", None, None),
        P("expert", None, None),
        P("expert", None, None),
    )
    return jax.shard_map(
        shards,
        mesh=mesh,
        in_specs=placed,
        out_specs=(
            P(("expert", "replica"), None),
            P("expert", None, "replica"),
            P("expert", None, "replica"),
            P("expert", "replica", None),
        ),
        check_vma=False,
    )
```

```python
import jax
import jax.numpy as jnp
from jax import lax
from jax.sharding import PartitionSpec as P

LANES = 128
CHUNKS = 4


def dequant(weight, scale):
    rows, cols = weight.shape
    srows, scols = scale.shape
    wide = jnp.repeat(scale, cols // scols, axis=1)
    blocks = weight.reshape(srows, rows // srows, cols).astype(jnp.float32)
    return (blocks * wide[:, None, :]).reshape(rows, cols).astype(jnp.bfloat16)


def forward_parts(xrows, gate_w, up_w):
    pre_gate = jnp.dot(xrows, gate_w, preferred_element_type=jnp.float32)
    pre_up = jnp.dot(xrows, up_w, preferred_element_type=jnp.float32)
    sig = jax.nn.sigmoid(pre_gate)
    act = pre_gate * sig
    return (pre_gate, pre_up, sig, act)


def unit_grads(row_grad, down_w, pre_gate, pre_up, sig, act):
    hidden_grad = jnp.dot(row_grad, down_w.T, preferred_element_type=jnp.float32)
    up_grad = (hidden_grad * act).astype(jnp.bfloat16)
    gate_grad = (hidden_grad * pre_up * sig * (1.0 + pre_gate * (1.0 - sig))).astype(jnp.bfloat16)
    return (gate_grad, up_grad)


def routing(expert_ids, gate_fixed, experts, capacity):
    tok_rows, topk = expert_ids.shape
    n = tok_rows * topk
    flat_ids = expert_ids.reshape(-1)
    onehot = flat_ids[:, None] == jnp.arange(experts, dtype=jnp.int32)[None, :]
    order = jnp.arange(n, dtype=jnp.int32)
    lower = (order[None, :] < order[:, None]).astype(jnp.bfloat16)
    before = jnp.dot(lower, onehot.astype(jnp.bfloat16), preferred_element_type=jnp.float32)
    slot_of = jnp.sum(jnp.where(onehot, before, 0.0), axis=1).astype(jnp.int32)
    dest = flat_ids * capacity + slot_of
    places = jnp.arange(experts * capacity, dtype=jnp.int32)
    pick = (dest[None, :] == places[:, None]).astype(jnp.bfloat16)
    flat_gate = gate_fixed.reshape(-1)
    token_of = order // topk
    cols = jnp.stack(
        [token_of, jnp.ones_like(token_of), flat_gate // 128, flat_gate % 128], axis=1
    ).astype(jnp.bfloat16)
    got = jnp.dot(pick, cols, preferred_element_type=jnp.float32)
    used = got[:, 1] > 0.5
    table = jnp.where(used, got[:, 0], float(tok_rows)).astype(jnp.int32)
    gate_table = (got[:, 2] * 128.0 + got[:, 3]) / 65536.0
    return flat_ids, slot_of, table, gate_table


def shards(
    x_quant, x_scale, out_grad, expert_ids, gate_fixed, w_gate, s_gate, w_up, s_up, w_down, s_down
):
    tok_rows, width = x_quant.shape
    topk = expert_ids.shape[1]
    experts = lax.axis_size("expert")
    capacity = tok_rows * topk * 5 // (4 * experts)
    chunks = CHUNKS if capacity % CHUNKS == 0 else 1
    per = capacity // chunks
    sub = width // LANES
    blk_width = width // x_scale.shape[1]
    flat_ids, slot_of, table, gate_table = routing(expert_ids, gate_fixed, experts, capacity)
    scaled = x_quant.reshape(tok_rows, -1, blk_width).astype(jnp.float32) * x_scale[:, :, None]
    inputs = scaled.reshape(tok_rows, sub, LANES).astype(jnp.bfloat16)
    zero_row = jnp.zeros((1, sub, LANES), jnp.bfloat16)
    source = jnp.concatenate(
        [inputs, zero_row, out_grad.reshape(tok_rows, sub, LANES), zero_row], axis=0
    )
    table = table.reshape(experts, capacity)
    gate_table = gate_table.reshape(experts, capacity)
    gate_w = dequant(w_gate[0], s_gate[0])
    up_w = dequant(w_up[0], s_up[0])
    down_w = dequant(w_down[0], s_down[0])
    rows_in = experts * per
    span = per * sub

    def payload_of(c):
        idx = table[:, c * per : (c + 1) * per]
        gates = gate_table[:, c * per : (c + 1) * per]
        both = jnp.concatenate([idx, idx + (tok_rows + 1)], axis=1)
        scale = jnp.concatenate([jnp.ones_like(gates), gates], axis=1)
        rows = (scale[:, :, None, None] * source[both].astype(jnp.float32)).astype(jnp.bfloat16)
        return [rows.reshape(experts, 2 * span, LANES)]

    both_w3 = jnp.concatenate([gate_w, up_w], axis=1).reshape(sub, LANES, -1)
    down_w3 = down_w.reshape(-1, sub, LANES)

    def compute(got):
        x3 = got[:, :span].reshape(rows_in, sub, LANES)
        g3 = got[:, span : 2 * span].reshape(rows_in, sub, LANES)
        pre = jnp.einsum("rkl,klf->rf", x3, both_w3, preferred_element_type=jnp.float32)
        ff = pre.shape[1] // 2
        pre_gate, pre_up = pre[:, :ff], pre[:, ff:]
        sig = jax.nn.sigmoid(pre_gate)
        act = pre_gate * sig
        hidden = (act * pre_up).astype(jnp.bfloat16)
        hidden_grad = jnp.einsum("rkl,fkl->rf", g3, down_w3, preferred_element_type=jnp.float32)
        up_grad = (hidden_grad * act).astype(jnp.bfloat16)
        gate_grad = (hidden_grad * pre_up * sig * (1.0 + pre_gate * (1.0 - sig))).astype(jnp.bfloat16)
        unit_grad = jnp.concatenate([gate_grad, up_grad], axis=1)
        row_input = jnp.einsum("rf,klf->rkl", unit_grad, both_w3, preferred_element_type=jnp.float32)
        back_rows = row_input.astype(jnp.bfloat16).reshape(experts, span, LANES)
        return back_rows, (x3.reshape(rows_in, width), g3.reshape(rows_in, width), hidden, gate_grad, up_grad)

    def weight_parts_of(group, r, half):
        xrows, row_grad, hidden, gate_grad, up_grad = group
        pick = lambda a: lax.dynamic_slice_in_dim(a, r * half, half, axis=1)
        part_gate = jnp.dot(xrows.T, pick(gate_grad), preferred_element_type=jnp.float32)
        part_up = jnp.dot(xrows.T, pick(up_grad), preferred_element_type=jnp.float32)
        part_down = jnp.dot(pick(hidden).T, row_grad, preferred_element_type=jnp.float32)
        return (part_gate, part_up, part_down)

    early_chunks = chunks - 1
    saved = []
    arrived = [None] * chunks
    backs = [None] * chunks
    returned = [None] * chunks
    for step in range(chunks + 2):
        pieces = []
        if step < chunks:
            pieces += payload_of(step)
        if step >= 2:
            pieces.append(backs[step - 2])
        got = lax.all_to_all(
            jnp.concatenate(pieces, axis=1), "expert", split_axis=0, concat_axis=0, tiled=True
        )
        if step < chunks:
            arrived[step] = got
        if step >= 2:
            returned[step - 2] = got[:, -span:]
        if 1 <= step <= chunks:
            backs[step - 1], kept = compute(arrived[step - 1])
            saved.append(kept)
        if step in (early_chunks - 1, early_chunks):
            first = 0 if step == early_chunks - 1 else early_chunks - 1
            early = tuple(jnp.concatenate(list(g), axis=0) for g in zip(*saved[first:]))
            half = early[3].shape[1] // lax.axis_size("replica")
            mine = lax.axis_index("replica")
            new_kept = weight_parts_of(early, mine, half)
            new_sent = weight_parts_of(early, 1 - mine, half)
            if first > 0:
                new_kept = tuple(a + b for a, b in zip(early_kept, new_kept))
                new_sent = tuple(a + b for a, b in zip(early_sent, new_sent))
            backs[step - 1], early_kept, early_sent = lax.optimization_barrier(
                (backs[step - 1], new_kept, new_sent)
            )
    ff = saved[0][3].shape[1]
    half = ff // lax.axis_size("replica")
    mine = lax.axis_index("replica")
    other = 1 - mine

    def cols(a, r):
        return lax.dynamic_slice_in_dim(a, r * half, half, axis=1)

    def weight_parts(group, r):
        xrows, row_grad, hidden, gate_grad, up_grad = group
        part_gate = jnp.dot(xrows.T, cols(gate_grad, r), preferred_element_type=jnp.float32)
        part_up = jnp.dot(xrows.T, cols(up_grad, r), preferred_element_type=jnp.float32)
        part_down = jnp.dot(cols(hidden, r).T, row_grad, preferred_element_type=jnp.float32)
        return (part_gate, part_up, part_down)

    late = tuple(jnp.concatenate(list(g), axis=0) for g in zip(*saved[early_chunks:]))
    late, _ = lax.optimization_barrier((late, returned[chunks - 2]))
    sent = tuple(
        (a + b).astype(jnp.bfloat16) for a, b in zip(early_sent, weight_parts(late, other))
    )
    kept = lax.optimization_barrier(
        tuple((a + b).astype(jnp.bfloat16) for a, b in zip(early_kept, weight_parts(late, mine)))
    )
    swap = [(0, 1), (1, 0)]
    came = tuple(lax.ppermute(p, "replica", swap) for p in sent)
    grad_gate, grad_up, grad_down = (
        (k.astype(jnp.float32) + c.astype(jnp.float32)).astype(jnp.bfloat16)[None]
        for k, c in zip(kept, came)
    )
    total = None
    for c in range(chunks):
        in_chunk = (slot_of // per) == c
        col = jnp.where(in_chunk, flat_ids * per + slot_of % per, -1)
        spots = jnp.arange(rows_in, dtype=jnp.int32)
        hit = (col[:, None] == spots[None, :]).astype(jnp.bfloat16)
        gather_mat = jnp.sum(hit.reshape(tok_rows, topk, rows_in), axis=1)
        back3 = returned[c].reshape(rows_in, sub, LANES)
        part = jnp.einsum("tj,jkl->tkl", gather_mat, back3, preferred_element_type=jnp.float32)
        total = part if total is None else total + part
    grad_input = total.reshape(tok_rows, width).astype(jnp.bfloat16)
    return (grad_input, grad_gate, grad_up, grad_down)


def solution(mesh):
    placed = (
        P(("expert", "replica"), None),
        P(("expert", "replica"), None),
        P(("expert", "replica"), None),
        P(("expert", "replica"), None),
        P(("expert", "replica"), None),
        P("expert", None, None),
        P("expert", None, None),
        P("expert", None, None),
        P("expert", None, None),
        P("expert", None, None),
        P("expert", None, None),
    )
    return jax.shard_map(
        shards,
        mesh=mesh,
        in_specs=placed,
        out_specs=(
            P(("expert", "replica"), None),
            P("expert", None, "replica"),
            P("expert", None, "replica"),
            P("expert", "replica", None),
        ),
        check_vma=False,
    )
```

```python
import jax
import jax.numpy as jnp
from jax import lax
from jax.sharding import PartitionSpec as P

LANES = 128
CHUNKS = 4


def dequant(weight, scale):
    rows, cols = weight.shape
    srows, scols = scale.shape
    wide = jnp.repeat(scale, cols // scols, axis=1)
    blocks = weight.reshape(srows, rows // srows, cols).astype(jnp.float32)
    return (blocks * wide[:, None, :]).reshape(rows, cols).astype(jnp.bfloat16)


def forward_parts(xrows, gate_w, up_w):
    pre_gate = jnp.dot(xrows, gate_w, preferred_element_type=jnp.float32)
    pre_up = jnp.dot(xrows, up_w, preferred_element_type=jnp.float32)
    sig = jax.nn.sigmoid(pre_gate)
    act = pre_gate * sig
    return (pre_gate, pre_up, sig, act)


def unit_grads(row_grad, down_w, pre_gate, pre_up, sig, act):
    hidden_grad = jnp.dot(row_grad, down_w.T, preferred_element_type=jnp.float32)
    up_grad = (hidden_grad * act).astype(jnp.bfloat16)
    gate_grad = (hidden_grad * pre_up * sig * (1.0 + pre_gate * (1.0 - sig))).astype(jnp.bfloat16)
    return (gate_grad, up_grad)


def routing(expert_ids, gate_fixed, experts, capacity):
    tok_rows, topk = expert_ids.shape
    n = tok_rows * topk
    flat_ids = expert_ids.reshape(-1)
    onehot = flat_ids[:, None] == jnp.arange(experts, dtype=jnp.int32)[None, :]
    order = jnp.arange(n, dtype=jnp.int32)
    lower = (order[None, :] < order[:, None]).astype(jnp.bfloat16)
    before = jnp.dot(lower, onehot.astype(jnp.bfloat16), preferred_element_type=jnp.float32)
    slot_of = jnp.sum(jnp.where(onehot, before, 0.0), axis=1).astype(jnp.int32)
    dest = flat_ids * capacity + slot_of
    places = jnp.arange(experts * capacity, dtype=jnp.int32)
    pick = (dest[None, :] == places[:, None]).astype(jnp.bfloat16)
    flat_gate = gate_fixed.reshape(-1)
    token_of = order // topk
    cols = jnp.stack(
        [token_of, jnp.ones_like(token_of), flat_gate // 128, flat_gate % 128], axis=1
    ).astype(jnp.bfloat16)
    got = jnp.dot(pick, cols, preferred_element_type=jnp.float32)
    used = got[:, 1] > 0.5
    table = jnp.where(used, got[:, 0], float(tok_rows)).astype(jnp.int32)
    gate_table = (got[:, 2] * 128.0 + got[:, 3]) / 65536.0
    return flat_ids, slot_of, table, gate_table


def shards(
    x_quant, x_scale, out_grad, expert_ids, gate_fixed, w_gate, s_gate, w_up, s_up, w_down, s_down
):
    tok_rows, width = x_quant.shape
    topk = expert_ids.shape[1]
    experts = lax.axis_size("expert")
    capacity = tok_rows * topk * 5 // (4 * experts)
    chunks = CHUNKS if capacity % CHUNKS == 0 else 1
    per = capacity // chunks
    sub = width // LANES
    blk_width = width // x_scale.shape[1]
    flat_ids, slot_of, table, gate_table = routing(expert_ids, gate_fixed, experts, capacity)
    scaled = x_quant.reshape(tok_rows, -1, blk_width).astype(jnp.float32) * x_scale[:, :, None]
    inputs = scaled.reshape(tok_rows, sub, LANES).astype(jnp.bfloat16)
    zero_row = jnp.zeros((1, sub, LANES), jnp.bfloat16)
    source = jnp.concatenate(
        [inputs, zero_row, out_grad.reshape(tok_rows, sub, LANES), zero_row], axis=0
    )
    table = table.reshape(experts, capacity)
    gate_table = gate_table.reshape(experts, capacity)
    gate_w = dequant(w_gate[0], s_gate[0])
    up_w = dequant(w_up[0], s_up[0])
    down_w = dequant(w_down[0], s_down[0])
    rows_in = experts * per
    span = per * sub

    def payload_of(c):
        idx = table[:, c * per : (c + 1) * per]
        gates = gate_table[:, c * per : (c + 1) * per]
        both = jnp.concatenate([idx, idx + (tok_rows + 1)], axis=1)
        scale = jnp.concatenate([jnp.ones_like(gates), gates], axis=1)
        rows = (scale[:, :, None, None] * source[both].astype(jnp.float32)).astype(jnp.bfloat16)
        return [rows.reshape(experts, 2 * span, LANES)]

    both_w3 = jnp.concatenate([gate_w, up_w], axis=1).reshape(sub, LANES, -1)
    down_w3 = down_w.reshape(-1, sub, LANES)

    def compute(got):
        x3 = got[:, :span].reshape(rows_in, sub, LANES)
        g3 = got[:, span : 2 * span].reshape(rows_in, sub, LANES)
        pre = jnp.einsum("rkl,klf->rf", x3, both_w3, preferred_element_type=jnp.float32)
        ff = pre.shape[1] // 2
        pre_gate, pre_up = pre[:, :ff], pre[:, ff:]
        sig = jax.nn.sigmoid(pre_gate)
        act = pre_gate * sig
        hidden = (act * pre_up).astype(jnp.bfloat16)
        hidden_grad = jnp.einsum("rkl,fkl->rf", g3, down_w3, preferred_element_type=jnp.float32)
        up_grad = (hidden_grad * act).astype(jnp.bfloat16)
        gate_grad = (hidden_grad * pre_up * sig * (1.0 + pre_gate * (1.0 - sig))).astype(jnp.bfloat16)
        unit_grad = jnp.concatenate([gate_grad, up_grad], axis=1)
        row_input = jnp.einsum("rf,klf->rkl", unit_grad, both_w3, preferred_element_type=jnp.float32)
        back_rows = row_input.astype(jnp.bfloat16).reshape(experts, span, LANES)
        return back_rows, (x3.reshape(rows_in, width), g3.reshape(rows_in, width), hidden, gate_grad, up_grad)

    def weight_parts_of(group, r, half):
        xrows, row_grad, hidden, gate_grad, up_grad = group
        pick = lambda a: lax.dynamic_slice_in_dim(a, r * half, half, axis=1)
        part_gate = jnp.dot(xrows.T, pick(gate_grad), preferred_element_type=jnp.float32)
        part_up = jnp.dot(xrows.T, pick(up_grad), preferred_element_type=jnp.float32)
        part_down = jnp.dot(pick(hidden).T, row_grad, preferred_element_type=jnp.float32)
        return (part_gate, part_up, part_down)

    early_chunks = chunks - 1
    saved = []
    arrived = [None] * chunks
    backs = [None] * chunks
    returned = [None] * chunks
    for step in range(chunks + 2):
        pieces = []
        if step < chunks:
            pieces += payload_of(step)
        if step >= 2:
            pieces.append(backs[step - 2])
        got = lax.all_to_all(
            jnp.concatenate(pieces, axis=1), "expert", split_axis=0, concat_axis=0, tiled=True
        )
        if step < chunks:
            arrived[step] = got
        if step >= 2:
            returned[step - 2] = got[:, -span:]
        if 1 <= step <= chunks:
            backs[step - 1], kept = compute(arrived[step - 1])
            saved.append(kept)
        if step in (early_chunks - 1, early_chunks):
            first = 0 if step == early_chunks - 1 else early_chunks - 2
            upto = early_chunks - 2 if step == early_chunks - 1 else early_chunks
            early = tuple(jnp.concatenate(list(g), axis=0) for g in zip(*saved[first:upto]))
            half = early[3].shape[1] // lax.axis_size("replica")
            mine = lax.axis_index("replica")
            new_kept = weight_parts_of(early, mine, half)
            new_sent = weight_parts_of(early, 1 - mine, half)
            if first > 0:
                new_kept = tuple(a + b for a, b in zip(early_kept, new_kept))
                new_sent = tuple(a + b for a, b in zip(early_sent, new_sent))
            backs[step - 1], early_kept, early_sent = lax.optimization_barrier(
                (backs[step - 1], new_kept, new_sent)
            )
    ff = saved[0][3].shape[1]
    half = ff // lax.axis_size("replica")
    mine = lax.axis_index("replica")
    other = 1 - mine

    def cols(a, r):
        return lax.dynamic_slice_in_dim(a, r * half, half, axis=1)

    def weight_parts(group, r):
        xrows, row_grad, hidden, gate_grad, up_grad = group
        part_gate = jnp.dot(xrows.T, cols(gate_grad, r), preferred_element_type=jnp.float32)
        part_up = jnp.dot(xrows.T, cols(up_grad, r), preferred_element_type=jnp.float32)
        part_down = jnp.dot(cols(hidden, r).T, row_grad, preferred_element_type=jnp.float32)
        return (part_gate, part_up, part_down)

    late = tuple(jnp.concatenate(list(g), axis=0) for g in zip(*saved[early_chunks:]))
    late, _ = lax.optimization_barrier((late, returned[chunks - 2]))
    sent = tuple(
        (a + b).astype(jnp.bfloat16) for a, b in zip(early_sent, weight_parts(late, other))
    )
    kept = lax.optimization_barrier(
        tuple((a + b).astype(jnp.bfloat16) for a, b in zip(early_kept, weight_parts(late, mine)))
    )
    swap = [(0, 1), (1, 0)]
    came = tuple(lax.ppermute(p, "replica", swap) for p in sent)
    grad_gate, grad_up, grad_down = (
        (k.astype(jnp.float32) + c.astype(jnp.float32)).astype(jnp.bfloat16)[None]
        for k, c in zip(kept, came)
    )
    total = None
    for c in range(chunks):
        in_chunk = (slot_of // per) == c
        col = jnp.where(in_chunk, flat_ids * per + slot_of % per, -1)
        spots = jnp.arange(rows_in, dtype=jnp.int32)
        hit = (col[:, None] == spots[None, :]).astype(jnp.bfloat16)
        gather_mat = jnp.sum(hit.reshape(tok_rows, topk, rows_in), axis=1)
        back3 = returned[c].reshape(rows_in, sub, LANES)
        part = jnp.einsum("tj,jkl->tkl", gather_mat, back3, preferred_element_type=jnp.float32)
        total = part if total is None else total + part
    grad_input = total.reshape(tok_rows, width).astype(jnp.bfloat16)
    return (grad_input, grad_gate, grad_up, grad_down)


def solution(mesh):
    placed = (
        P(("expert", "replica"), None),
        P(("expert", "replica"), None),
        P(("expert", "replica"), None),
        P(("expert", "replica"), None),
        P(("expert", "replica"), None),
        P("expert", None, None),
        P("expert", None, None),
        P("expert", None, None),
        P("expert", None, None),
        P("expert", None, None),
        P("expert", None, None),
    )
    return jax.shard_map(
        shards,
        mesh=mesh,
        in_specs=placed,
        out_specs=(
            P(("expert", "replica"), None),
            P("expert", None, "replica"),
            P("expert", None, "replica"),
            P("expert", "replica", None),
        ),
        check_vma=False,
    )
```
